256 devices in a mesh: seq: 32 (over z, y), tp: 8 (over x, core).
Axes of the slice: x: 4, y: 4, z: 8, core: 2. Of those that a mesh axis runs over, the one named last changes fastest.
Arguments:
- tokens: bfloat16 [4096, 2048], P('seq'), may hold values from -6 to 6
- norm_gain: float32 [2048], replicated, may hold values from 0.5 to 1.5
- w_x: bfloat16 [2048, 2048], P(None, 'tp'), may hold values from -0.125 to 0.125
- w_z: bfloat16 [2048, 2048], P(None, 'tp'), may hold values from -0.125 to 0.125
- conv_w: float32 [4, 2048], P(None, 'tp'), may hold values from -3 to 3
- conv_b: float32 [2048], P('tp'), may hold values from -0.5 to 0.5
- w_xproj: bfloat16 [2048, 160], P('tp'), may hold values from -0.125 to 0.125
- w_dt: bfloat16 [128, 2048], P(None, 'tp'), may hold values from -0.5 to 0.5
- dt_bias: float32 [2048], P('tp'), may hold values from -4.6 to -3.4
- a_log: float32 [16, 2048], P(None, 'tp'), may hold values from -3.9 to -0.7
- d_skip: float32 [2048], P('tp'), may hold values from 0.5 to 1.5
- w_out: bfloat16 [2048, 2048], P('tp'), may hold values from -0.125 to 0.125
- mlp_gain: float32 [2048], replicated, may hold values from 0.5 to 1.5
- w_gate: bfloat16 [2048, 4096], P(None, 'tp'), may hold values from -0.125 to 0.125
- w_up: bfloat16 [2048, 4096], P(None, 'tp'), may hold values from -0.125 to 0.125
- w_down: bfloat16 [4096, 2048], P('tp'), may hold values from -0.09375 to 0.09375
- prompt_lengths: int32 [16], replicated, may hold values from 1 to 2048, as said below
- request_prompt: int32 [128], P('seq'), may hold values from 0 to 15, as said below
Outputs:
- mixed_out: bfloat16 [4096, 2048], P(('seq', 'tp'))
- req_states: float32 [128, 16, 2048], P('seq', None, 'tp')
- req_edges: bfloat16 [128, 3, 2048], P('seq', None, 'tp')
The draws below stay inside these ranges and needn't reach their ends.
Inputs may be any that keep to these rules, and one draw needn't show every extreme that they name: `prompt_lengths`: the prompts are packed in order from slot 0 and sum to 4032 tokens; the remaining slots are padding; the last prompt is exactly 2048 long. `request_prompt`: every prompt is continued by at least one request.
All inputs are finite; a program needn't handle non-finite values.
Results may differ from the reference program's by a relative error of at most 0.025.
Values may be sent and summed in bfloat16 or wider, within the bound.
No kernel may reach another device: no remote copies, remote signals or barrier semaphores. Data moves between devices by JAX's collectives and lax.ppermute only.
A program may use at most 64 MiB of HBM per device.

```python
import jax
import jax.numpy as jnp
from jax import lax

D = 2048
E = 2048
N = 16
K = 4
R = 128
FF = 4096
BLOCK = 128
TOKENS = 4096
PROMPTS = 16
LEN_MAX = 2048
REQ = 128
N_TP = 8


def draw_prompt_lengths(key, part):
    total_len = TOKENS - BLOCK // 2
    key_order, key_weight = jax.random.split(jax.random.fold_in(key, 3), 2)
    shuffled = jax.random.permutation(key_order, PROMPTS).astype(jnp.int32)
    long_index = PROMPTS - 1
    short_index = jnp.where(shuffled[0] == long_index, shuffled[1], shuffled[0])
    prompt_ids = jnp.arange(PROMPTS, dtype=jnp.int32)
    others = (prompt_ids != long_index) & (prompt_ids != short_index)
    weights = jnp.where(others, jax.random.randint(key_weight, (PROMPTS,), 1, 5, dtype=jnp.int32), 0)
    spread_left = total_len - LEN_MAX - 1 - (PROMPTS - 2)
    shares = spread_left * weights // jnp.sum(weights)
    leftover = spread_left - jnp.sum(shares)
    rank_among = jnp.cumsum(others.astype(jnp.int32)) - 1
    extra_one = (others & (rank_among < leftover)).astype(jnp.int32)
    lengths = jnp.where(others, 1 + shares + extra_one, 0)
    lengths = lengths + jnp.where(prompt_ids == long_index, LEN_MAX, 0) + jnp.where(prompt_ids == short_index, 1, 0)
    return lengths.astype(jnp.int32)


def draw_request_prompt(key, part):
    key_pick, key_place = jax.random.split(jax.random.fold_in(key, 7), 2)
    picked = jax.random.randint(key_pick, (REQ,), 0, PROMPTS, dtype=jnp.int32)
    placed = jax.random.permutation(key_place, REQ)[:PROMPTS]
    return picked.at[placed].set(jnp.arange(PROMPTS, dtype=jnp.int32)).astype(jnp.int32)


def block_scale(stream_key, shape, cuts, least, high):
    def one(axis_at, shards_of):
        heights = jax.random.uniform(jax.random.fold_in(jax.random.fold_in(stream_key, 6), axis_at), (shards_of,), jnp.float32, least / len(cuts), high / len(cuts))
        return jnp.repeat(jnp.exp(heights), shape[axis_at] // shards_of).reshape((-1,) + (1,) * (len(shape) - axis_at - 1))

    level = one(*cuts[0])
    for cut in cuts[1:]:
        level = level * one(*cut)
    return level


def bell_draw(rng, dims, width, bound, cuts=(), kind=jnp.bfloat16):
    entries = width * jax.random.normal(rng, dims, jnp.float32)
    if cuts:
        entries = entries * block_scale(rng, dims, cuts, -0.22, 0.18)
    return jnp.clip(entries, -bound, bound).astype(kind)


def setup_inputs(seed: int = 0) -> dict:
    splits = jax.random.split(jax.random.key(seed), 19)
    tokens = bell_draw(splits[0], (TOKENS, D), 1.0, 6.0, ((0, 32),))
    norm_gain = jnp.clip(1.0 + 0.1 * jax.random.normal(splits[1], (D,), jnp.float32), 0.5, 1.5)
    w_x = bell_draw(splits[2], (D, E), D ** -0.5, 0.125, ((1, 8),))
    w_z = bell_draw(splits[3], (D, E), D ** -0.5, 0.125, ((1, 8),))
    conv_w = bell_draw(splits[4], (K, E), K ** -0.5, 3.0, ((1, 8),), jnp.float32)
    conv_b = jnp.clip(jax.random.uniform(splits[5], (E,), jnp.float32, -0.5, 0.5) * block_scale(splits[5], (E,), ((0, 8),), -0.4, 0.0), -0.5, 0.5)
    w_xproj = bell_draw(splits[6], (E, R + 2 * N), E ** -0.5, 0.125, ((0, 8),))
    w_dt = bell_draw(splits[7], (R, E), R ** -0.5, 0.5, ((1, 8),))
    dt_bias = jnp.clip(-4.6 + 1.1999998 * jax.random.uniform(splits[8], (E,), jnp.float32) ** block_scale(splits[8], (E,), ((0, 8),), -0.2, 0.2), -4.6, -3.4)
    a_log = jnp.clip(-3.9 + 3.2 * jax.random.uniform(splits[9], (N, E), jnp.float32) ** block_scale(splits[9], (N, E), ((1, 8),), -0.2, 0.2), -3.9, -0.7)
    d_skip = jnp.clip(0.5 + 1.0 * jax.random.uniform(splits[10], (E,), jnp.float32) ** block_scale(splits[10], (E,), ((0, 8),), -0.2, 0.2), 0.5, 1.5)
    w_out = bell_draw(splits[11], (E, D), E ** -0.5, 0.125, ((0, 8),))
    mlp_gain = jnp.clip(1.0 + 0.1 * jax.random.normal(splits[12], (D,), jnp.float32), 0.5, 1.5)
    w_gate = bell_draw(splits[13], (D, FF), D ** -0.5, 0.125, ((1, 8),))
    w_up = bell_draw(splits[14], (D, FF), D ** -0.5, 0.125, ((1, 8),))
    w_down = bell_draw(splits[15], (FF, D), FF ** -0.5, 0.09375, ((0, 8),))
    prompt_lengths = draw_prompt_lengths(jax.random.fold_in(splits[18], 71), 0)
    request_prompt = draw_request_prompt(jax.random.fold_in(splits[18], 71), 0)
    return {"tokens": tokens, "norm_gain": norm_gain, "w_x": w_x, "w_z": w_z, "conv_w": conv_w, "conv_b": conv_b, "w_xproj": w_xproj, "w_dt": w_dt, "dt_bias": dt_bias, "a_log": a_log, "d_skip": d_skip, "w_out": w_out, "mlp_gain": mlp_gain, "w_gate": w_gate, "w_up": w_up, "w_down": w_down, "prompt_lengths": prompt_lengths, "request_prompt": request_prompt}


EPSILON = 1e-05

def rms_norm(values, gain):
    scale = lax.rsqrt(lax.optimization_barrier(jnp.mean(values * values, axis=-1, keepdims=True)) + EPSILON)
    return values * scale * gain.astype(jnp.float32)

def grouped_product(left, right, groups):
    group_width = left.shape[1] // groups
    running_sum = jnp.zeros((left.shape[0], right.shape[1]), jnp.float32)
    for group_index in range(groups):
        lower = group_index * group_width
        upper = lower + group_width
        part_value = jnp.dot(left[:, lower:upper], right[lower:upper], preferred_element_type=jnp.float32).astype(jnp.bfloat16)
        part_value = lax.optimization_barrier(part_value)
        running_sum = running_sum + part_value.astype(jnp.float32)
    return running_sum

def reference(tokens, norm_gain, w_x, w_z, conv_w, conv_b, w_xproj, w_dt, dt_bias, a_log, d_skip, w_out, mlp_gain, w_gate, w_up, w_down, prompt_lengths, request_prompt):
    places = jnp.arange(TOKENS, dtype=jnp.int32)
    prompt_end = jnp.cumsum(prompt_lengths).astype(jnp.int32)
    prompt_start = (prompt_end - prompt_lengths).astype(jnp.int32)
    prompt_ids = jnp.arange(PROMPTS, dtype=jnp.int32)
    prompt_of = lax.optimization_barrier(jnp.sum((places[:, None] >= prompt_end[None, :]).astype(jnp.int32), axis=1))
    start_of = lax.optimization_barrier(jnp.sum(jnp.where(prompt_of[:, None] == prompt_ids[None, :], prompt_start[None, :], 0), axis=1)).astype(jnp.int32)
    offset = places - start_of
    starts_here = jnp.any(places[:, None] == prompt_start[None, :], axis=1)
    ends_here = jnp.any(places[:, None] == prompt_end[None, :] - 1, axis=1)
    is_live = prompt_of < PROMPTS
    normed = rms_norm(tokens.astype(jnp.float32), norm_gain).astype(jnp.bfloat16)
    x_branch = jnp.dot(normed, w_x, preferred_element_type=jnp.float32).astype(jnp.bfloat16)
    z_branch = jnp.dot(normed, w_z, preferred_element_type=jnp.float32).astype(jnp.bfloat16)
    edge_len = K - 1
    padded = jnp.concatenate([jnp.zeros((edge_len, E), jnp.bfloat16), x_branch], axis=0)
    conv_sum = jnp.zeros((TOKENS, E), jnp.float32) + conv_b.astype(jnp.float32)[None, :]
    for lag_steps in range(K):
        window = padded[edge_len - lag_steps:edge_len - lag_steps + TOKENS].astype(jnp.float32)
        reach_mask = (offset >= lag_steps).astype(jnp.float32)[:, None]
        conv_sum = conv_sum + conv_w[edge_len - lag_steps].astype(jnp.float32)[None, :] * window * reach_mask
    conv_out = jax.nn.silu(conv_sum).astype(jnp.bfloat16)
    projected = jnp.dot(conv_out, w_xproj, preferred_element_type=jnp.float32)
    low_rank = projected[:, :R].astype(jnp.bfloat16)
    in_map = projected[:, R:R + N]
    out_map = projected[:, R + N:]
    step_size = jax.nn.softplus(jnp.dot(low_rank, w_dt, preferred_element_type=jnp.float32) + dt_bias.astype(jnp.float32)[None, :])
    decay_rates = -jnp.exp(a_log.astype(jnp.float32))
    driven = step_size * conv_out.astype(jnp.float32)
    carry_on = 1.0 - starts_here.astype(jnp.float32)
    slot_of = jnp.minimum(prompt_of, PROMPTS - 1).astype(jnp.int32)

    def advance(carry, inputs):
        state, finals = carry
        step_now, driven_now, in_now, out_now, keep_now, end_now, slot_now = inputs
        state = jnp.exp(step_now[None, :] * decay_rates) * keep_now * state + driven_now[None, :] * in_now[:, None]
        finals = finals.at[slot_now].add(state * end_now)
        return ((state, finals), lax.optimization_barrier(jnp.sum(out_now[:, None] * state, axis=0)))
    start_carry = (jnp.zeros((N, E), jnp.float32), jnp.zeros((PROMPTS, N, E), jnp.float32))
    scanned = (step_size, driven, in_map, out_map, carry_on, ends_here.astype(jnp.float32), slot_of)
    (last_state, finals), mixer_y = lax.scan(advance, start_carry, scanned)
    mixer_y = mixer_y + d_skip.astype(jnp.float32)[None, :] * conv_out.astype(jnp.float32)
    gated = (mixer_y * jax.nn.silu(z_branch.astype(jnp.float32))).astype(jnp.bfloat16)
    residual = tokens.astype(jnp.float32) + grouped_product(gated, w_out, N_TP)
    normed_two = rms_norm(residual, mlp_gain).astype(jnp.bfloat16)
    gate_val = jnp.dot(normed_two, w_gate, preferred_element_type=jnp.float32)
    up_val = jnp.dot(normed_two, w_up, preferred_element_type=jnp.float32)
    hidden = (jax.nn.silu(gate_val) * up_val).astype(jnp.bfloat16)
    summed = residual + grouped_product(hidden, w_down, N_TP)
    mixed_out = (summed * is_live.astype(jnp.float32)[:, None]).astype(jnp.bfloat16)
    lag_ids = jnp.arange(edge_len, dtype=jnp.int32)
    target = prompt_end[:, None] - edge_len + lag_ids[None, :]
    inside = target >= prompt_start[:, None]
    edge_rows = jnp.where(inside[:, :, None], x_branch[jnp.maximum(target, 0)], jnp.zeros((), jnp.bfloat16))
    req_states = finals[request_prompt]
    req_edges = edge_rows[request_prompt]
    return (mixed_out, req_states, req_edges)
```

```python
import functools

import jax
import jax.numpy as jnp
from jax import lax
from jax.experimental import pallas as pl
from jax.experimental.pallas import tpu as pltpu
from jax.sharding import PartitionSpec as P

EPSILON = 1e-05
INTERPRET = False


def from_behind(x, axis, by):
    devices = lax.axis_size(axis)
    pairs = [(i, i + by) for i in range(devices) if 0 <= i + by < devices]
    return lax.ppermute(x, axis, pairs)


def swap(x, axis, bit):
    devices = lax.axis_size(axis)
    return lax.ppermute(x, axis, [(i, i ^ bit) for i in range(devices)])


def bits_of(devices):
    out = []
    bit = 1
    while bit < devices:
        out.append(bit)
        bit *= 2
    assert bit == devices
    return out


def butterfly_sum(x, axis, send_dtype):
    for bit in bits_of(lax.axis_size(axis)):
        x = x + swap(x.astype(send_dtype), axis, bit).astype(x.dtype)
    return x


def scatter_rows(x, axis, first_dtype):
    devices = lax.axis_size(axis)
    bits = bits_of(devices)
    me = lax.axis_index(axis)
    depth = len(bits)
    rows = x.shape[0] // devices
    buf = x.reshape((2,) * depth + (rows, x.shape[1]))
    send_dtype = first_dtype
    for level, bit in enumerate(bits):
        at = depth - 1 - level
        mine = ((me // bit) % 2).astype(jnp.int32)
        keep = lax.dynamic_index_in_dim(buf, mine, at, False)
        give = lax.dynamic_index_in_dim(buf, 1 - mine, at, False)
        got = swap(give.astype(send_dtype), axis, bit)
        buf = keep.astype(jnp.float32) + got.astype(jnp.float32)
        send_dtype = jnp.float32
    return buf


def gather_rows(x, axis):
    devices = lax.axis_size(axis)
    bits = bits_of(devices)
    me = lax.axis_index(axis)
    buf = x
    for level, bit in enumerate(reversed(bits)):
        got = swap(buf, axis, bit)
        upper = ((me // bit) % 2) == 1
        low = jnp.where(upper, got, buf)
        high = jnp.where(upper, buf, got)
        buf = jnp.stack([low, high], axis=level)
    return buf.reshape((devices * x.shape[0], x.shape[1]))


def rms_norm(values, gain):
    scale = lax.rsqrt(jnp.mean(values * values, axis=-1, keepdims=True) + EPSILON)
    return values * scale * gain


def block_summary_kernel(da_ref, dr_ref, send_ref, atot_ref):
    steps = da_ref.shape[0]

    def chunk(c, carry):
        state, acum = carry
        base = c * 8
        for i in range(8):
            da = da_ref[base + i]
            state = da * state + dr_ref[base + i]
            acum = da * acum
        return state, acum

    zero = jnp.zeros(send_ref.shape, jnp.float32)
    one = jnp.ones(atot_ref.shape, jnp.float32)
    state, acum = lax.fori_loop(0, steps // 8, chunk, (zero, one))
    send_ref[...] = state
    atot_ref[...] = acum


def block_output_kernel(da_ref, dr_ref, om_ref, sin_ref, endf_ref, pid_ref, y_ref, fin_ref):
    steps = da_ref.shape[0]
    width = y_ref.shape[1]
    fin_ref[...] = jnp.zeros(fin_ref.shape, jnp.float32)
    row_ids = lax.broadcasted_iota(jnp.int32, (8, width), 0)

    def chunk(c, state):
        base = pl.multiple_of(c * 8, 8)
        rows = jnp.zeros((8, width), jnp.float32)
        for i in range(8):
            t = base + i
            state = da_ref[t] * state + dr_ref[t]
            here = jnp.sum(om_ref[t] * state, axis=0, keepdims=True)
            rows = jnp.where(row_ids == i, here, rows)

            @pl.when(endf_ref[t] != 0)
            def _():
                fin_ref[pid_ref[t]] = state

        y_ref[pl.ds(base, 8), :] = rows
        return state

    lax.fori_loop(0, steps // 8, chunk, sin_ref[...])


def block_summary(da, dr):
    _, n, e = da.shape
    vmem = pl.BlockSpec(memory_space=pltpu.VMEM)
    return pl.pallas_call(
        block_summary_kernel,
        out_shape=(
            jax.ShapeDtypeStruct((n, e), jnp.float32),
            jax.ShapeDtypeStruct((n, e), jnp.float32),
        ),
        in_specs=[vmem, vmem],
        out_specs=(vmem, vmem),
        interpret=INTERPRET,
    )(da, dr)


def block_output(da, dr, om, sin, endf, pid, prompts):
    t, n, e = da.shape
    vmem = pl.BlockSpec(memory_space=pltpu.VMEM)
    smem = pl.BlockSpec(memory_space=pltpu.SMEM)
    return pl.pallas_call(
        block_output_kernel,
        out_shape=(
            jax.ShapeDtypeStruct((t, e), jnp.float32),
            jax.ShapeDtypeStruct((prompts, n, e), jnp.float32),
        ),
        in_specs=[vmem, vmem, vmem, vmem, smem, smem],
        out_specs=(vmem, vmem),
        interpret=INTERPRET,
    )(da, dr, om, sin, endf, pid)


def entering_state(a_blk, s_blk, axis):
    me = lax.axis_index(axis)
    devices = lax.axis_size(axis)
    inc_a, inc_s = a_blk, s_blk
    exc_a, exc_s = jnp.ones_like(a_blk), jnp.zeros_like(s_blk)
    shift = 1
    while shift < devices:
        got = from_behind(jnp.stack([inc_a, inc_s]), axis, shift)
        got_a, got_s = got[0], got[1]
        has = me >= shift
        new_exc_a = got_a * exc_a
        new_exc_s = exc_a * got_s + exc_s
        new_inc_a = got_a * inc_a
        new_inc_s = inc_a * got_s + inc_s
        exc_a = jnp.where(has, new_exc_a, exc_a)
        exc_s = jnp.where(has, new_exc_s, exc_s)
        inc_a = jnp.where(has, new_inc_a, inc_a)
        inc_s = jnp.where(has, new_inc_s, inc_s)
        shift *= 2
    return exc_s


def local(
    tokens,
    norm_gain,
    w_x,
    w_z,
    conv_w,
    conv_b,
    w_xproj,
    w_dt,
    dt_bias,
    a_log,
    d_skip,
    w_out,
    mlp_gain,
    w_gate,
    w_up,
    w_down,
    prompt_lengths,
    request_prompt,
):
    block_len = tokens.shape[0]
    tp_count = lax.axis_size("tp")
    row_count = block_len // tp_count
    seq_pos = lax.axis_index("seq")
    tp_pos = lax.axis_index("tp")
    first_row = seq_pos * block_len
    prompts = prompt_lengths.shape[0]
    kernel_len = conv_w.shape[0]
    edge_len = kernel_len - 1
    low_dim = w_dt.shape[0]
    state_dim = a_log.shape[0]
    chans = w_x.shape[1]
    places = first_row + jnp.arange(block_len, dtype=jnp.int32)
    prompt_end = jnp.cumsum(prompt_lengths)
    prompt_start = prompt_end - prompt_lengths
    prompt_ids = jnp.arange(prompts, dtype=jnp.int32)
    prompt_of = jnp.sum((places[:, None] >= prompt_end[None, :]).astype(jnp.int32), axis=1)
    start_of = jnp.sum(
        jnp.where(prompt_of[:, None] == prompt_ids[None, :], prompt_start[None, :], 0), axis=1
    )
    offset = places - start_of
    starts_here = jnp.any(places[:, None] == prompt_start[None, :], axis=1)
    ends_here = jnp.any(places[:, None] == prompt_end[None, :] - 1, axis=1)
    is_live = prompt_of < prompts
    normed = rms_norm(tokens.astype(jnp.float32), norm_gain).astype(jnp.bfloat16)
    x_branch = jnp.dot(normed, w_x, preferred_element_type=jnp.float32).astype(jnp.bfloat16)
    z_branch = jnp.dot(normed, w_z, preferred_element_type=jnp.float32).astype(jnp.bfloat16)
    carried = from_behind(x_branch[block_len - edge_len :], "seq", 1)
    extended = jnp.concatenate([carried, x_branch], axis=0)
    conv_sum = jnp.zeros((block_len, chans), jnp.float32) + conv_b[None, :]
    for lag_steps in range(kernel_len):
        window = extended[edge_len - lag_steps : edge_len - lag_steps + block_len].astype(
            jnp.float32
        )
        reach_mask = (offset >= lag_steps).astype(jnp.float32)[:, None]
        conv_sum = conv_sum + conv_w[edge_len - lag_steps][None, :] * window * reach_mask
    conv_out = jax.nn.silu(conv_sum).astype(jnp.bfloat16)
    conv_float = conv_out.astype(jnp.float32)
    projected = butterfly_sum(
        jnp.dot(conv_out, w_xproj, preferred_element_type=jnp.float32), "tp", jnp.float32
    )
    low_rank = projected[:, :low_dim].astype(jnp.bfloat16)
    in_map = projected[:, low_dim : low_dim + state_dim]
    out_map = projected[:, low_dim + state_dim :]
    step_size = jax.nn.softplus(
        jnp.dot(low_rank, w_dt, preferred_element_type=jnp.float32) + dt_bias[None, :]
    )
    decay_rates = -jnp.exp(a_log)
    carry_on = 1.0 - starts_here.astype(jnp.float32)
    decay = jnp.exp(step_size[:, None, :] * decay_rates[None, :, :]) * carry_on[:, None, None]
    drive = (step_size * conv_float)[:, None, :] * in_map[:, :, None]
    out_wide = jnp.broadcast_to(out_map[:, :, None], decay.shape)
    s_blk, a_blk = block_summary(decay, drive)
    state_in = entering_state(a_blk, s_blk, "seq")
    end_flag = ends_here.astype(jnp.int32)
    slot_of = jnp.minimum(prompt_of, prompts - 1).astype(jnp.int32)
    mixer_y, final_part = block_output(decay, drive, out_wide, state_in, end_flag, slot_of, prompts)
    mixer_y = mixer_y + d_skip[None, :] * conv_float
    gated = (mixer_y * jax.nn.silu(z_branch.astype(jnp.float32))).astype(jnp.bfloat16)
    ends_local = (prompt_end - 1 >= first_row) & (prompt_end - 1 < first_row + block_len)
    lag_ids = jnp.arange(edge_len, dtype=jnp.int32)
    ext_rows = jnp.arange(block_len + edge_len, dtype=jnp.int32)
    target_row = prompt_end[:, None] + lag_ids[None, :] - first_row
    inside = (
        prompt_end[:, None] - edge_len + lag_ids[None, :] >= prompt_start[:, None]
    ) & ends_local[:, None]
    edge_pick = ((ext_rows[None, None, :] == target_row[:, :, None]) & inside[:, :, None]).astype(
        jnp.bfloat16
    )
    edge_part = jnp.einsum("pji,ie->pje", edge_pick, extended, preferred_element_type=jnp.float32)
    handed = jnp.concatenate(
        [final_part.astype(jnp.bfloat16), edge_part.astype(jnp.bfloat16)], axis=1
    )
    handed = butterfly_sum(handed, "seq", jnp.bfloat16).astype(jnp.float32)
    final_all = handed[:, :state_dim]
    edge_all = handed[:, state_dim:]
    chooser = (request_prompt[:, None] == prompt_ids[None, :]).astype(jnp.float32)
    req_states = jnp.einsum("rp,pne->rne", chooser, final_all, precision=lax.Precision.HIGHEST)
    req_edges = jnp.einsum(
        "rp,pje->rje", chooser, edge_all, precision=lax.Precision.HIGHEST
    ).astype(jnp.bfloat16)
    mixed_rows = scatter_rows(
        jnp.dot(gated, w_out, preferred_element_type=jnp.float32).astype(jnp.bfloat16),
        "tp",
        jnp.bfloat16,
    )
    token_rows = lax.dynamic_slice_in_dim(tokens, tp_pos * row_count, row_count, 0)
    residual_rows = token_rows.astype(jnp.float32) + mixed_rows
    normed_rows = rms_norm(residual_rows, mlp_gain).astype(jnp.bfloat16)
    normed_two = gather_rows(normed_rows, "tp")
    gate_val = jnp.dot(normed_two, w_gate, preferred_element_type=jnp.float32)
    up_val = jnp.dot(normed_two, w_up, preferred_element_type=jnp.float32)
    hidden = (jax.nn.silu(gate_val) * up_val).astype(jnp.bfloat16)
    mlp_share = scatter_rows(
        jnp.dot(hidden, w_down, preferred_element_type=jnp.float32).astype(jnp.bfloat16),
        "tp",
        jnp.bfloat16,
    )
    live_rows = lax.dynamic_slice_in_dim(is_live, tp_pos * row_count, row_count, 0).astype(
        jnp.float32
    )
    mixed_out = ((residual_rows + mlp_share) * live_rows[:, None]).astype(jnp.bfloat16)
    return (mixed_out, req_states, req_edges)


def solution(mesh):
    placed = (
        P("seq", None),
        P(),
        P(None, "tp"),
        P(None, "tp"),
        P(None, "tp"),
        P("tp"),
        P("tp", None),
        P(None, "tp"),
        P("tp"),
        P(None, "tp"),
        P("tp"),
        P("tp", None),
        P(),
        P(None, "tp"),
        P(None, "tp"),
        P("tp", None),
        P(),
        P("seq"),
    )
    return jax.shard_map(
        local,
        mesh=mesh,
        in_specs=placed,
        out_specs=(P(("seq", "tp"), None), P("seq", None, "tp"), P("seq", None, "tp")),
        check_vma=False,
    )
```

```python
import functools

import jax
import jax.numpy as jnp
from jax import lax
from jax.experimental import pallas as pl
from jax.experimental.pallas import tpu as pltpu
from jax.sharding import PartitionSpec as P

EPSILON = 1e-05
INTERPRET = False


def from_behind(x, axis, by):
    devices = lax.axis_size(axis)
    pairs = [(i, i + by) for i in range(devices) if 0 <= i + by < devices]
    return lax.ppermute(x, axis, pairs)


def swap(x, axis, bit):
    devices = lax.axis_size(axis)
    return lax.ppermute(x, axis, [(i, i ^ bit) for i in range(devices)])


def bits_of(devices):
    out = []
    bit = 1
    while bit < devices:
        out.append(bit)
        bit *= 2
    assert bit == devices
    return out


def butterfly_sum(x, axis, send_dtype):
    for bit in bits_of(lax.axis_size(axis)):
        x = x + swap(x.astype(send_dtype), axis, bit).astype(x.dtype)
    return x


def scatter_rows(x, axis, first_dtype):
    devices = lax.axis_size(axis)
    bits = bits_of(devices)
    me = lax.axis_index(axis)
    depth = len(bits)
    rows = x.shape[0] // devices
    buf = x.reshape((2,) * depth + (rows, x.shape[1]))
    send_dtype = first_dtype
    for level, bit in enumerate(bits):
        at = depth - 1 - level
        mine = ((me // bit) % 2).astype(jnp.int32)
        keep = lax.dynamic_index_in_dim(buf, mine, at, False)
        give = lax.dynamic_index_in_dim(buf, 1 - mine, at, False)
        got = swap(give.astype(send_dtype), axis, bit)
        buf = keep.astype(jnp.float32) + got.astype(jnp.float32)
        send_dtype = jnp.float32
    return buf


def gather_rows(x, axis):
    devices = lax.axis_size(axis)
    bits = bits_of(devices)
    me = lax.axis_index(axis)
    buf = x
    for level, bit in enumerate(reversed(bits)):
        got = swap(buf, axis, bit)
        upper = ((me // bit) % 2) == 1
        low = jnp.where(upper, got, buf)
        high = jnp.where(upper, buf, got)
        buf = jnp.stack([low, high], axis=level)
    return buf.reshape((devices * x.shape[0], x.shape[1]))


def rms_norm(values, gain):
    scale = lax.rsqrt(jnp.mean(values * values, axis=-1, keepdims=True) + EPSILON)
    return values * scale * gain


def block_summary_kernel(da_ref, dr_ref, send_ref, atot_ref):
    steps = da_ref.shape[0]

    def chunk(c, carry):
        state, acum = carry
        base = c * 8
        for i in range(8):
            da = da_ref[base + i]
            state = da * state + dr_ref[base + i]
            acum = da * acum
        return state, acum

    zero = jnp.zeros(send_ref.shape, jnp.float32)
    one = jnp.ones(atot_ref.shape, jnp.float32)
    state, acum = lax.fori_loop(0, steps // 8, chunk, (zero, one))
    send_ref[...] = state
    atot_ref[...] = acum


def block_output_kernel(da_ref, dr_ref, om_ref, sin_ref, endf_ref, pid_ref, y_ref, fin_ref):
    steps = da_ref.shape[0]
    width = y_ref.shape[1]
    fin_ref[...] = jnp.zeros(fin_ref.shape, jnp.float32)
    row_ids = lax.broadcasted_iota(jnp.int32, (8, width), 0)

    def chunk(c, state):
        base = pl.multiple_of(c * 8, 8)
        rows = jnp.zeros((8, width), jnp.float32)
        for i in range(8):
            t = base + i
            state = da_ref[t] * state + dr_ref[t]
            here = jnp.sum(om_ref[t] * state, axis=0, keepdims=True)
            rows = jnp.where(row_ids == i, here, rows)

            @pl.when(endf_ref[t] != 0)
            def _():
                fin_ref[pid_ref[t]] = state

        y_ref[pl.ds(base, 8), :] = rows
        return state

    lax.fori_loop(0, steps // 8, chunk, sin_ref[...])


def block_summary(da, dr):
    _, n, e = da.shape
    vmem = pl.BlockSpec(memory_space=pltpu.VMEM)
    return pl.pallas_call(
        block_summary_kernel,
        out_shape=(
            jax.ShapeDtypeStruct((n, e), jnp.float32),
            jax.ShapeDtypeStruct((n, e), jnp.float32),
        ),
        in_specs=[vmem, vmem],
        out_specs=(vmem, vmem),
        interpret=INTERPRET,
    )(da, dr)


def block_output(da, dr, om, sin, endf, pid, prompts):
    t, n, e = da.shape
    vmem = pl.BlockSpec(memory_space=pltpu.VMEM)
    smem = pl.BlockSpec(memory_space=pltpu.SMEM)
    return pl.pallas_call(
        block_output_kernel,
        out_shape=(
            jax.ShapeDtypeStruct((t, e), jnp.float32),
            jax.ShapeDtypeStruct((prompts, n, e), jnp.float32),
        ),
        in_specs=[vmem, vmem, vmem, vmem, smem, smem],
        out_specs=(vmem, vmem),
        interpret=INTERPRET,
    )(da, dr, om, sin, endf, pid)


def entering_state(a_blk, s_blk, axis):
    me = lax.axis_index(axis)
    devices = lax.axis_size(axis)
    inc_a, inc_s = a_blk, s_blk
    exc_a, exc_s = jnp.ones_like(a_blk), jnp.zeros_like(s_blk)
    span = 1
    while span < devices:
        radix = min(8, devices // span)
        pack = jnp.stack([inc_a, inc_s])
        got = [from_behind(pack, axis, span * j) for j in range(radix - 1, 0, -1)]
        acc_a, acc_s = jnp.ones_like(a_blk), jnp.zeros_like(s_blk)
        for j, one in zip(range(radix - 1, 0, -1), got):
            has = me >= span * j
            acc_s = jnp.where(has, one[0] * acc_s + one[1], acc_s)
            acc_a = jnp.where(has, one[0] * acc_a, acc_a)
        exc_a, exc_s = acc_a * exc_a, exc_a * acc_s + exc_s
        inc_a, inc_s = acc_a * inc_a, inc_a * acc_s + inc_s
        span *= radix
    return exc_s


def local(
    tokens,
    norm_gain,
    w_x,
    w_z,
    conv_w,
    conv_b,
    w_xproj,
    w_dt,
    dt_bias,
    a_log,
    d_skip,
    w_out,
    mlp_gain,
    w_gate,
    w_up,
    w_down,
    prompt_lengths,
    request_prompt,
):
    block_len = tokens.shape[0]
    tp_count = lax.axis_size("tp")
    row_count = block_len // tp_count
    seq_pos = lax.axis_index("seq")
    tp_pos = lax.axis_index("tp")
    first_row = seq_pos * block_len
    prompts = prompt_lengths.shape[0]
    kernel_len = conv_w.shape[0]
    edge_len = kernel_len - 1
    low_dim = w_dt.shape[0]
    state_dim = a_log.shape[0]
    chans = w_x.shape[1]
    places = first_row + jnp.arange(block_len, dtype=jnp.int32)
    prompt_end = jnp.cumsum(prompt_lengths)
    prompt_start = prompt_end - prompt_lengths
    prompt_ids = jnp.arange(prompts, dtype=jnp.int32)
    prompt_of = jnp.sum((places[:, None] >= prompt_end[None, :]).astype(jnp.int32), axis=1)
    start_of = jnp.sum(
        jnp.where(prompt_of[:, None] == prompt_ids[None, :], prompt_start[None, :], 0), axis=1
    )
    offset = places - start_of
    starts_here = jnp.any(places[:, None] == prompt_start[None, :], axis=1)
    ends_here = jnp.any(places[:, None] == prompt_end[None, :] - 1, axis=1)
    is_live = prompt_of < prompts
    normed = rms_norm(tokens.astype(jnp.float32), norm_gain).astype(jnp.bfloat16)
    x_branch = jnp.dot(normed, w_x, preferred_element_type=jnp.float32).astype(jnp.bfloat16)
    z_branch = jnp.dot(normed, w_z, preferred_element_type=jnp.float32).astype(jnp.bfloat16)
    carried = from_behind(x_branch[block_len - edge_len :], "seq", 1)
    extended = jnp.concatenate([carried, x_branch], axis=0)
    conv_sum = jnp.zeros((block_len, chans), jnp.float32) + conv_b[None, :]
    for lag_steps in range(kernel_len):
        window = extended[edge_len - lag_steps : edge_len - lag_steps + block_len].astype(
            jnp.float32
        )
        reach_mask = (offset >= lag_steps).astype(jnp.float32)[:, None]
        conv_sum = conv_sum + conv_w[edge_len - lag_steps][None, :] * window * reach_mask
    conv_out = jax.nn.silu(conv_sum).astype(jnp.bfloat16)
    conv_float = conv_out.astype(jnp.float32)
    projected = butterfly_sum(
        jnp.dot(conv_out, w_xproj, preferred_element_type=jnp.float32), "tp", jnp.float32
    )
    low_rank = projected[:, :low_dim].astype(jnp.bfloat16)
    in_map = projected[:, low_dim : low_dim + state_dim]
    out_map = projected[:, low_dim + state_dim :]
    step_size = jax.nn.softplus(
        jnp.dot(low_rank, w_dt, preferred_element_type=jnp.float32) + dt_bias[None, :]
    )
    decay_rates = -jnp.exp(a_log)
    carry_on = 1.0 - starts_here.astype(jnp.float32)
    decay = jnp.exp(step_size[:, None, :] * decay_rates[None, :, :]) * carry_on[:, None, None]
    drive = (step_size * conv_float)[:, None, :] * in_map[:, :, None]
    out_wide = jnp.broadcast_to(out_map[:, :, None], decay.shape)
    s_blk, a_blk = block_summary(decay, drive)
    state_in = entering_state(a_blk, s_blk, "seq")
    end_flag = ends_here.astype(jnp.int32)
    slot_of = jnp.minimum(prompt_of, prompts - 1).astype(jnp.int32)
    mixer_y, final_part = block_output(decay, drive, out_wide, state_in, end_flag, slot_of, prompts)
    mixer_y = mixer_y + d_skip[None, :] * conv_float
    gated = (mixer_y * jax.nn.silu(z_branch.astype(jnp.float32))).astype(jnp.bfloat16)
    ends_local = (prompt_end - 1 >= first_row) & (prompt_end - 1 < first_row + block_len)
    lag_ids = jnp.arange(edge_len, dtype=jnp.int32)
    ext_rows = jnp.arange(block_len + edge_len, dtype=jnp.int32)
    target_row = prompt_end[:, None] + lag_ids[None, :] - first_row
    inside = (
        prompt_end[:, None] - edge_len + lag_ids[None, :] >= prompt_start[:, None]
    ) & ends_local[:, None]
    edge_pick = ((ext_rows[None, None, :] == target_row[:, :, None]) & inside[:, :, None]).astype(
        jnp.bfloat16
    )
    edge_part = jnp.einsum("pji,ie->pje", edge_pick, extended, preferred_element_type=jnp.float32)
    handed = jnp.concatenate(
        [final_part.astype(jnp.bfloat16), edge_part.astype(jnp.bfloat16)], axis=1
    )
    mixed_rows = scatter_rows(
        jnp.dot(gated, w_out, preferred_element_type=jnp.float32).astype(jnp.bfloat16),
        "tp",
        jnp.bfloat16,
    )
    token_rows = lax.dynamic_slice_in_dim(tokens, tp_pos * row_count, row_count, 0)
    residual_rows = token_rows.astype(jnp.float32) + mixed_rows
    normed_rows = rms_norm(residual_rows, mlp_gain).astype(jnp.bfloat16)
    normed_two = gather_rows(normed_rows, "tp")
    gate_val = jnp.dot(normed_two, w_gate, preferred_element_type=jnp.float32)
    up_val = jnp.dot(normed_two, w_up, preferred_element_type=jnp.float32)
    hidden = (jax.nn.silu(gate_val) * up_val).astype(jnp.bfloat16)
    mlp_share = scatter_rows(
        jnp.dot(hidden, w_down, preferred_element_type=jnp.float32).astype(jnp.bfloat16),
        "tp",
        jnp.bfloat16,
    )
    handed, mlp_share = lax.optimization_barrier((handed, mlp_share))
    handed = butterfly_sum(handed, "seq", jnp.bfloat16).astype(jnp.float32)
    final_all = handed[:, :state_dim]
    edge_all = handed[:, state_dim:]
    chooser = (request_prompt[:, None] == prompt_ids[None, :]).astype(jnp.float32)
    req_states = jnp.einsum("rp,pne->rne", chooser, final_all, precision=lax.Precision.HIGHEST)
    req_edges = jnp.einsum(
        "rp,pje->rje", chooser, edge_all, precision=lax.Precision.HIGHEST
    ).astype(jnp.bfloat16)
    live_rows = lax.dynamic_slice_in_dim(is_live, tp_pos * row_count, row_count, 0).astype(
        jnp.float32
    )
    mixed_out = ((residual_rows + mlp_share) * live_rows[:, None]).astype(jnp.bfloat16)
    return (mixed_out, req_states, req_edges)


def solution(mesh):
    placed = (
        P("seq", None),
        P(),
        P(None, "tp"),
        P(None, "tp"),
        P(None, "tp"),
        P("tp"),
        P("tp", None),
        P(None, "tp"),
        P("tp"),
        P(None, "tp"),
        P("tp"),
        P("tp", None),
        P(),
        P(None, "tp"),
        P(None, "tp"),
        P("tp", None),
        P(),
        P("seq"),
    )
    return jax.shard_map(
        local,
        mesh=mesh,
        in_specs=placed,
        out_specs=(P(("seq", "tp"), None), P("seq", None, "tp"), P("seq", None, "tp")),
        check_vma=False,
    )
```

```python
import functools

import jax
import jax.numpy as jnp
from jax import lax
from jax.experimental import pallas as pl
from jax.experimental.pallas import tpu as pltpu
from jax.sharding import PartitionSpec as P

EPSILON = 1e-05
INTERPRET = False


def from_behind(x, axis, by):
    devices = lax.axis_size(axis)
    pairs = [(i, i + by) for i in range(devices) if 0 <= i + by < devices]
    return lax.ppermute(x, axis, pairs)


def swap(x, axis, bit):
    devices = lax.axis_size(axis)
    return lax.ppermute(x, axis, [(i, i ^ bit) for i in range(devices)])


def bits_of(devices):
    out = []
    bit = 1
    while bit < devices:
        out.append(bit)
        bit *= 2
    assert bit == devices
    return out


def butterfly_sum(x, axis, send_dtype):
    for bit in bits_of(lax.axis_size(axis)):
        x = x + swap(x.astype(send_dtype), axis, bit).astype(x.dtype)
    return x


def scatter_rows(x, axis, first_dtype):
    devices = lax.axis_size(axis)
    bits = bits_of(devices)
    me = lax.axis_index(axis)
    depth = len(bits)
    rows = x.shape[0] // devices
    buf = x.reshape((2,) * depth + (rows, x.shape[1]))
    send_dtype = first_dtype
    for level, bit in enumerate(bits):
        at = depth - 1 - level
        mine = ((me // bit) % 2).astype(jnp.int32)
        keep = lax.dynamic_index_in_dim(buf, mine, at, False)
        give = lax.dynamic_index_in_dim(buf, 1 - mine, at, False)
        got = swap(give.astype(send_dtype), axis, bit)
        buf = keep.astype(jnp.float32) + got.astype(jnp.float32)
    return buf


def gather_rows(x, axis):
    devices = lax.axis_size(axis)
    bits = bits_of(devices)
    me = lax.axis_index(axis)
    buf = x
    for level, bit in enumerate(reversed(bits)):
        got = swap(buf, axis, bit)
        upper = ((me // bit) % 2) == 1
        low = jnp.where(upper, got, buf)
        high = jnp.where(upper, buf, got)
        buf = jnp.stack([low, high], axis=level)
    return buf.reshape((devices * x.shape[0], x.shape[1]))


def rms_norm(values, gain):
    scale = lax.rsqrt(jnp.mean(values * values, axis=-1, keepdims=True) + EPSILON)
    return values * scale * gain


def block_summary_kernel(da_ref, dr_ref, send_ref, atot_ref):
    steps = da_ref.shape[0]

    def chunk(c, carry):
        state, acum = carry
        base = c * 8
        for i in range(8):
            da = da_ref[base + i]
            state = da * state + dr_ref[base + i]
            acum = da * acum
        return state, acum

    zero = jnp.zeros(send_ref.shape, jnp.float32)
    one = jnp.ones(atot_ref.shape, jnp.float32)
    state, acum = lax.fori_loop(0, steps // 8, chunk, (zero, one))
    send_ref[...] = state
    atot_ref[...] = acum


def block_output_kernel(da_ref, dr_ref, om_ref, sin_ref, endf_ref, pid_ref, y_ref, fin_ref):
    steps = da_ref.shape[0]
    width = y_ref.shape[1]
    fin_ref[...] = jnp.zeros(fin_ref.shape, jnp.float32)
    row_ids = lax.broadcasted_iota(jnp.int32, (8, width), 0)

    def chunk(c, state):
        base = pl.multiple_of(c * 8, 8)
        rows = jnp.zeros((8, width), jnp.float32)
        for i in range(8):
            t = base + i
            state = da_ref[t] * state + dr_ref[t]
            here = jnp.sum(om_ref[t] * state, axis=0, keepdims=True)
            rows = jnp.where(row_ids == i, here, rows)

            @pl.when(endf_ref[t] != 0)
            def _():
                fin_ref[pid_ref[t]] = state

        y_ref[pl.ds(base, 8), :] = rows
        return state

    lax.fori_loop(0, steps // 8, chunk, sin_ref[...])


def block_summary(da, dr):
    _, n, e = da.shape
    vmem = pl.BlockSpec(memory_space=pltpu.VMEM)
    return pl.pallas_call(
        block_summary_kernel,
        out_shape=(
            jax.ShapeDtypeStruct((n, e), jnp.float32),
            jax.ShapeDtypeStruct((n, e), jnp.float32),
        ),
        in_specs=[vmem, vmem],
        out_specs=(vmem, vmem),
        interpret=INTERPRET,
    )(da, dr)


def block_output(da, dr, om, sin, endf, pid, prompts):
    t, n, e = da.shape
    vmem = pl.BlockSpec(memory_space=pltpu.VMEM)
    smem = pl.BlockSpec(memory_space=pltpu.SMEM)
    return pl.pallas_call(
        block_output_kernel,
        out_shape=(
            jax.ShapeDtypeStruct((t, e), jnp.float32),
            jax.ShapeDtypeStruct((prompts, n, e), jnp.float32),
        ),
        in_specs=[vmem, vmem, vmem, vmem, smem, smem],
        out_specs=(vmem, vmem),
        interpret=INTERPRET,
    )(da, dr, om, sin, endf, pid)


def entering_state(a_blk, s_blk, axis):
    me = lax.axis_index(axis)
    devices = lax.axis_size(axis)
    inc_a, inc_s = a_blk, s_blk
    exc_a, exc_s = jnp.ones_like(a_blk), jnp.zeros_like(s_blk)
    shift = 1
    while shift < devices:
        got = from_behind(jnp.stack([inc_a, inc_s]), axis, shift)
        got_a, got_s = got[0], got[1]
        has = me >= shift
        new_exc_a = got_a * exc_a
        new_exc_s = exc_a * got_s + exc_s
        new_inc_a = got_a * inc_a
        new_inc_s = inc_a * got_s + inc_s
        exc_a = jnp.where(has, new_exc_a, exc_a)
        exc_s = jnp.where(has, new_exc_s, exc_s)
        inc_a = jnp.where(has, new_inc_a, inc_a)
        inc_s = jnp.where(has, new_inc_s, inc_s)
        shift *= 2
    return exc_s


def local(
    tokens,
    norm_gain,
    w_x,
    w_z,
    conv_w,
    conv_b,
    w_xproj,
    w_dt,
    dt_bias,
    a_log,
    d_skip,
    w_out,
    mlp_gain,
    w_gate,
    w_up,
    w_down,
    prompt_lengths,
    request_prompt,
):
    block_len = tokens.shape[0]
    tp_count = lax.axis_size("tp")
    row_count = block_len // tp_count
    seq_pos = lax.axis_index("seq")
    tp_pos = lax.axis_index("tp")
    first_row = seq_pos * block_len
    prompts = prompt_lengths.shape[0]
    kernel_len = conv_w.shape[0]
    edge_len = kernel_len - 1
    low_dim = w_dt.shape[0]
    state_dim = a_log.shape[0]
    chans = w_x.shape[1]
    places = first_row + jnp.arange(block_len, dtype=jnp.int32)
    prompt_end = jnp.cumsum(prompt_lengths)
    prompt_start = prompt_end - prompt_lengths
    prompt_ids = jnp.arange(prompts, dtype=jnp.int32)
    prompt_of = jnp.sum((places[:, None] >= prompt_end[None, :]).astype(jnp.int32), axis=1)
    start_of = jnp.sum(
        jnp.where(prompt_of[:, None] == prompt_ids[None, :], prompt_start[None, :], 0), axis=1
    )
    offset = places - start_of
    starts_here = jnp.any(places[:, None] == prompt_start[None, :], axis=1)
    ends_here = jnp.any(places[:, None] == prompt_end[None, :] - 1, axis=1)
    is_live = prompt_of < prompts
    behind = from_behind(tokens[block_len - edge_len :], "seq", 1)
    normed = rms_norm(tokens.astype(jnp.float32), norm_gain).astype(jnp.bfloat16)
    normed_behind = rms_norm(behind.astype(jnp.float32), norm_gain).astype(jnp.bfloat16)
    x_branch = jnp.dot(normed, w_x, preferred_element_type=jnp.float32).astype(jnp.bfloat16)
    z_branch = jnp.dot(normed, w_z, preferred_element_type=jnp.float32).astype(jnp.bfloat16)
    x_behind = jnp.dot(normed_behind, w_x, preferred_element_type=jnp.float32).astype(jnp.bfloat16)
    extended = jnp.concatenate([x_behind, x_branch], axis=0)
    conv_sum = jnp.zeros((block_len, chans), jnp.float32) + conv_b[None, :]
    for lag_steps in range(kernel_len):
        window = extended[edge_len - lag_steps : edge_len - lag_steps + block_len].astype(
            jnp.float32
        )
        reach_mask = (offset >= lag_steps).astype(jnp.float32)[:, None]
        conv_sum = conv_sum + conv_w[edge_len - lag_steps][None, :] * window * reach_mask
    conv_out = jax.nn.silu(conv_sum).astype(jnp.bfloat16)
    conv_float = conv_out.astype(jnp.float32)
    projected = butterfly_sum(
        jnp.dot(conv_out, w_xproj, preferred_element_type=jnp.float32), "tp", jnp.float32
    )
    low_rank = projected[:, :low_dim].astype(jnp.bfloat16)
    in_map = projected[:, low_dim : low_dim + state_dim]
    out_map = projected[:, low_dim + state_dim :]
    step_size = jax.nn.softplus(
        jnp.dot(low_rank, w_dt, preferred_element_type=jnp.float32) + dt_bias[None, :]
    )
    decay_rates = -jnp.exp(a_log)
    carry_on = 1.0 - starts_here.astype(jnp.float32)
    decay = jnp.exp(step_size[:, None, :] * decay_rates[None, :, :]) * carry_on[:, None, None]
    drive = (step_size * conv_float)[:, None, :] * in_map[:, :, None]
    out_wide = jnp.broadcast_to(out_map[:, :, None], decay.shape)
    s_blk, a_blk = block_summary(decay, drive)
    state_in = entering_state(a_blk, s_blk, "seq")
    end_flag = ends_here.astype(jnp.int32)
    slot_of = jnp.minimum(prompt_of, prompts - 1).astype(jnp.int32)
    mixer_y, final_part = block_output(decay, drive, out_wide, state_in, end_flag, slot_of, prompts)
    mixer_y = mixer_y + d_skip[None, :] * conv_float
    gated = (mixer_y * jax.nn.silu(z_branch.astype(jnp.float32))).astype(jnp.bfloat16)
    ends_local = (prompt_end - 1 >= first_row) & (prompt_end - 1 < first_row + block_len)
    lag_ids = jnp.arange(edge_len, dtype=jnp.int32)
    ext_rows = jnp.arange(block_len + edge_len, dtype=jnp.int32)
    target_row = prompt_end[:, None] + lag_ids[None, :] - first_row
    inside = (
        prompt_end[:, None] - edge_len + lag_ids[None, :] >= prompt_start[:, None]
    ) & ends_local[:, None]
    edge_pick = ((ext_rows[None, None, :] == target_row[:, :, None]) & inside[:, :, None]).astype(
        jnp.bfloat16
    )
    edge_part = jnp.einsum("pji,ie->pje", edge_pick, extended, preferred_element_type=jnp.float32)
    handed = jnp.concatenate(
        [final_part.astype(jnp.bfloat16), edge_part.astype(jnp.bfloat16)], axis=1
    )
    handed = butterfly_sum(handed, "seq", jnp.bfloat16).astype(jnp.float32)
    final_all = handed[:, :state_dim]
    edge_all = handed[:, state_dim:]
    chooser = (request_prompt[:, None] == prompt_ids[None, :]).astype(jnp.float32)
    req_states = jnp.einsum("rp,pne->rne", chooser, final_all, precision=lax.Precision.HIGHEST)
    req_edges = jnp.einsum(
        "rp,pje->rje", chooser, edge_all, precision=lax.Precision.HIGHEST
    ).astype(jnp.bfloat16)
    mixed_rows = scatter_rows(
        jnp.dot(gated, w_out, preferred_element_type=jnp.float32).astype(jnp.bfloat16),
        "tp",
        jnp.bfloat16,
    )
    token_rows = lax.dynamic_slice_in_dim(tokens, tp_pos * row_count, row_count, 0)
    residual_rows = token_rows.astype(jnp.float32) + mixed_rows
    normed_rows = rms_norm(residual_rows, mlp_gain).astype(jnp.bfloat16)
    normed_two = gather_rows(normed_rows, "tp")
    gate_val = jnp.dot(normed_two, w_gate, preferred_element_type=jnp.float32)
    up_val = jnp.dot(normed_two, w_up, preferred_element_type=jnp.float32)
    hidden = (jax.nn.silu(gate_val) * up_val).astype(jnp.bfloat16)
    mlp_share = scatter_rows(
        jnp.dot(hidden, w_down, preferred_element_type=jnp.float32).astype(jnp.bfloat16),
        "tp",
        jnp.bfloat16,
    )
    live_rows = lax.dynamic_slice_in_dim(is_live, tp_pos * row_count, row_count, 0).astype(
        jnp.float32
    )
    mixed_out = ((residual_rows + mlp_share) * live_rows[:, None]).astype(jnp.bfloat16)
    return (mixed_out, req_states, req_edges)


def solution(mesh):
    placed = (
        P("seq", None),
        P(),
        P(None, "tp"),
        P(None, "tp"),
        P(None, "tp"),
        P("tp"),
        P("tp", None),
        P(None, "tp"),
        P("tp"),
        P(None, "tp"),
        P("tp"),
        P("tp", None),
        P(),
        P(None, "tp"),
        P(None, "tp"),
        P("tp", None),
        P(),
        P("seq"),
    )
    return jax.shard_map(
        local,
        mesh=mesh,
        in_specs=placed,
        out_specs=(P(("seq", "tp"), None), P("seq", None, "tp"), P("seq", None, "tp")),
        check_vma=False,
    )
```

```python
import functools

import jax
import jax.numpy as jnp
from jax import lax
from jax.experimental import pallas as pl
from jax.experimental.pallas import tpu as pltpu
from jax.sharding import PartitionSpec as P

EPSILON = 1e-05
INTERPRET = False


def from_behind(x, axis, by):
    devices = lax.axis_size(axis)
    pairs = [(i, i + by) for i in range(devices) if 0 <= i + by < devices]
    return lax.ppermute(x, axis, pairs)


def swap(x, axis, bit):
    devices = lax.axis_size(axis)
    return lax.ppermute(x, axis, [(i, i ^ bit) for i in range(devices)])


def bits_of(devices):
    out = []
    bit = 1
    while bit < devices:
        out.append(bit)
        bit *= 2
    assert bit == devices
    return out


def butterfly_sum(x, axis, send_dtype):
    for bit in bits_of(lax.axis_size(axis)):
        x = x + swap(x.astype(send_dtype), axis, bit).astype(x.dtype)
    return x


def scatter_rows(x, axis, first_dtype):
    devices = lax.axis_size(axis)
    bits = bits_of(devices)
    me = lax.axis_index(axis)
    depth = len(bits)
    rows = x.shape[0] // devices
    buf = x.reshape((2,) * depth + (rows, x.shape[1]))
    send_dtype = first_dtype
    for level, bit in enumerate(bits):
        at = depth - 1 - level
        mine = ((me // bit) % 2).astype(jnp.int32)
        keep = lax.dynamic_index_in_dim(buf, mine, at, False)
        give = lax.dynamic_index_in_dim(buf, 1 - mine, at, False)
        got = swap(give.astype(send_dtype), axis, bit)
        buf = keep.astype(jnp.float32) + got.astype(jnp.float32)
    return buf


def gather_rows(x, axis):
    devices = lax.axis_size(axis)
    bits = bits_of(devices)
    me = lax.axis_index(axis)
    buf = x
    for level, bit in enumerate(reversed(bits)):
        got = swap(buf, axis, bit)
        upper = ((me // bit) % 2) == 1
        low = jnp.where(upper, got, buf)
        high = jnp.where(upper, buf, got)
        buf = jnp.stack([low, high], axis=level)
    return buf.reshape((devices * x.shape[0], x.shape[1]))


def rms_norm(values, gain):
    scale = lax.rsqrt(jnp.mean(values * values, axis=-1, keepdims=True) + EPSILON)
    return values * scale * gain


def block_summary_kernel(da_ref, dr_ref, send_ref, atot_ref):
    steps = da_ref.shape[0]

    def chunk(c, carry):
        state, acum = carry
        base = c * 8
        for i in range(8):
            da = da_ref[base + i]
            state = da * state + dr_ref[base + i]
            acum = da * acum
        return state, acum

    zero = jnp.zeros(send_ref.shape, jnp.float32)
    one = jnp.ones(atot_ref.shape, jnp.float32)
    state, acum = lax.fori_loop(0, steps // 8, chunk, (zero, one))
    send_ref[...] = state
    atot_ref[...] = acum


def block_local_kernel(da_ref, dr_ref, om_ref, endf_ref, pid_ref, y_ref, g_ref, fs_ref, fd_ref):
    steps = da_ref.shape[0]
    width = y_ref.shape[1]
    fs_ref[...] = jnp.zeros(fs_ref.shape, jnp.float32)
    fd_ref[...] = jnp.zeros(fd_ref.shape, jnp.float32)
    row_ids = lax.broadcasted_iota(jnp.int32, (8, width), 0)

    def chunk(c, carry):
        state, acum = carry
        base = pl.multiple_of(c * 8, 8)
        rows = jnp.zeros((8, width), jnp.float32)
        for i in range(8):
            t = base + i
            da = da_ref[t]
            state = da * state + dr_ref[t]
            acum = da * acum
            om = om_ref[t]
            here = jnp.sum(om * state, axis=0, keepdims=True)
            rows = jnp.where(row_ids == i, here, rows)
            g_ref[t] = om * acum

            @pl.when(endf_ref[t] != 0)
            def _():
                fs_ref[pid_ref[t]] = state
                fd_ref[pid_ref[t]] = acum

        y_ref[pl.ds(base, 8), :] = rows
        return state, acum

    zero = jnp.zeros(fs_ref.shape[1:], jnp.float32)
    one = jnp.ones(fd_ref.shape[1:], jnp.float32)
    lax.fori_loop(0, steps // 8, chunk, (zero, one))


def block_summary(da, dr):
    _, n, e = da.shape
    vmem = pl.BlockSpec(memory_space=pltpu.VMEM)
    return pl.pallas_call(
        block_summary_kernel,
        out_shape=(
            jax.ShapeDtypeStruct((n, e), jnp.float32),
            jax.ShapeDtypeStruct((n, e), jnp.float32),
        ),
        in_specs=[vmem, vmem],
        out_specs=(vmem, vmem),
        interpret=INTERPRET,
    )(da, dr)


def block_local(da, dr, om, endf, pid, prompts):
    t, n, e = da.shape
    vmem = pl.BlockSpec(memory_space=pltpu.VMEM)
    smem = pl.BlockSpec(memory_space=pltpu.SMEM)
    return pl.pallas_call(
        block_local_kernel,
        out_shape=(
            jax.ShapeDtypeStruct((t, e), jnp.float32),
            jax.ShapeDtypeStruct((t, n, e), jnp.float32),
            jax.ShapeDtypeStruct((prompts, n, e), jnp.float32),
            jax.ShapeDtypeStruct((prompts, n, e), jnp.float32),
        ),
        in_specs=[vmem, vmem, vmem, smem, smem],
        out_specs=(vmem, vmem, vmem, vmem),
        interpret=INTERPRET,
    )(da, dr, om, endf, pid)


def entering_state(a_blk, s_blk, axis):
    me = lax.axis_index(axis)
    devices = lax.axis_size(axis)
    inc_a, inc_s = a_blk, s_blk
    exc_a, exc_s = jnp.ones_like(a_blk), jnp.zeros_like(s_blk)
    shift = 1
    while shift < devices:
        got = from_behind(jnp.stack([inc_a, inc_s]), axis, shift)
        got_a, got_s = got[0], got[1]
        has = me >= shift
        new_exc_a = got_a * exc_a
        new_exc_s = exc_a * got_s + exc_s
        new_inc_a = got_a * inc_a
        new_inc_s = inc_a * got_s + inc_s
        exc_a = jnp.where(has, new_exc_a, exc_a)
        exc_s = jnp.where(has, new_exc_s, exc_s)
        inc_a = jnp.where(has, new_inc_a, inc_a)
        inc_s = jnp.where(has, new_inc_s, inc_s)
        shift *= 2
    return exc_s


def local(
    tokens,
    norm_gain,
    w_x,
    w_z,
    conv_w,
    conv_b,
    w_xproj,
    w_dt,
    dt_bias,
    a_log,
    d_skip,
    w_out,
    mlp_gain,
    w_gate,
    w_up,
    w_down,
    prompt_lengths,
    request_prompt,
):
    block_len = tokens.shape[0]
    tp_count = lax.axis_size("tp")
    row_count = block_len // tp_count
    seq_pos = lax.axis_index("seq")
    tp_pos = lax.axis_index("tp")
    first_row = seq_pos * block_len
    prompts = prompt_lengths.shape[0]
    kernel_len = conv_w.shape[0]
    edge_len = kernel_len - 1
    low_dim = w_dt.shape[0]
    state_dim = a_log.shape[0]
    chans = w_x.shape[1]
    places = first_row + jnp.arange(block_len, dtype=jnp.int32)
    prompt_end = jnp.cumsum(prompt_lengths)
    prompt_start = prompt_end - prompt_lengths
    prompt_ids = jnp.arange(prompts, dtype=jnp.int32)
    prompt_of = jnp.sum((places[:, None] >= prompt_end[None, :]).astype(jnp.int32), axis=1)
    start_of = jnp.sum(
        jnp.where(prompt_of[:, None] == prompt_ids[None, :], prompt_start[None, :], 0), axis=1
    )
    offset = places - start_of
    starts_here = jnp.any(places[:, None] == prompt_start[None, :], axis=1)
    ends_here = jnp.any(places[:, None] == prompt_end[None, :] - 1, axis=1)
    is_live = prompt_of < prompts
    behind = from_behind(tokens[block_len - edge_len :], "seq", 1)
    normed = rms_norm(tokens.astype(jnp.float32), norm_gain).astype(jnp.bfloat16)
    normed_behind = rms_norm(behind.astype(jnp.float32), norm_gain).astype(jnp.bfloat16)
    x_branch = jnp.dot(normed, w_x, preferred_element_type=jnp.float32).astype(jnp.bfloat16)
    z_branch = jnp.dot(normed, w_z, preferred_element_type=jnp.float32).astype(jnp.bfloat16)
    x_behind = jnp.dot(normed_behind, w_x, preferred_element_type=jnp.float32).astype(jnp.bfloat16)
    extended = jnp.concatenate([x_behind, x_branch], axis=0)
    conv_sum = jnp.zeros((block_len, chans), jnp.float32) + conv_b[None, :]
    for lag_steps in range(kernel_len):
        window = extended[edge_len - lag_steps : edge_len - lag_steps + block_len].astype(
            jnp.float32
        )
        reach_mask = (offset >= lag_steps).astype(jnp.float32)[:, None]
        conv_sum = conv_sum + conv_w[edge_len - lag_steps][None, :] * window * reach_mask
    conv_out = jax.nn.silu(conv_sum).astype(jnp.bfloat16)
    conv_float = conv_out.astype(jnp.float32)
    projected = butterfly_sum(
        jnp.dot(conv_out, w_xproj, preferred_element_type=jnp.float32), "tp", jnp.float32
    )
    low_rank = projected[:, :low_dim].astype(jnp.bfloat16)
    in_map = projected[:, low_dim : low_dim + state_dim]
    out_map = projected[:, low_dim + state_dim :]
    step_size = jax.nn.softplus(
        jnp.dot(low_rank, w_dt, preferred_element_type=jnp.float32) + dt_bias[None, :]
    )
    decay_rates = -jnp.exp(a_log)
    carry_on = 1.0 - starts_here.astype(jnp.float32)
    decay = jnp.exp(step_size[:, None, :] * decay_rates[None, :, :]) * carry_on[:, None, None]
    drive = (step_size * conv_float)[:, None, :] * in_map[:, :, None]
    out_wide = jnp.broadcast_to(out_map[:, :, None], decay.shape)
    s_blk, a_blk = block_summary(decay, drive)
    end_flag = ends_here.astype(jnp.int32)
    slot_of = jnp.minimum(prompt_of, prompts - 1).astype(jnp.int32)
    y_zero, g_share, end_state, end_decay = block_local(
        decay, drive, out_wide, end_flag, slot_of, prompts
    )
    state_in = entering_state(a_blk, s_blk, "seq")
    mixer_y = y_zero + jnp.sum(g_share * state_in[None], axis=1)
    final_part = end_state + end_decay * state_in[None]
    mixer_y = mixer_y + d_skip[None, :] * conv_float
    gated = (mixer_y * jax.nn.silu(z_branch.astype(jnp.float32))).astype(jnp.bfloat16)
    ends_local = (prompt_end - 1 >= first_row) & (prompt_end - 1 < first_row + block_len)
    lag_ids = jnp.arange(edge_len, dtype=jnp.int32)
    ext_rows = jnp.arange(block_len + edge_len, dtype=jnp.int32)
    target_row = prompt_end[:, None] + lag_ids[None, :] - first_row
    inside = (
        prompt_end[:, None] - edge_len + lag_ids[None, :] >= prompt_start[:, None]
    ) & ends_local[:, None]
    edge_pick = ((ext_rows[None, None, :] == target_row[:, :, None]) & inside[:, :, None]).astype(
        jnp.bfloat16
    )
    edge_part = jnp.einsum("pji,ie->pje", edge_pick, extended, preferred_element_type=jnp.float32)
    handed = jnp.concatenate(
        [final_part.astype(jnp.bfloat16), edge_part.astype(jnp.bfloat16)], axis=1
    )
    handed = butterfly_sum(handed, "seq", jnp.bfloat16).astype(jnp.float32)
    final_all = handed[:, :state_dim]
    edge_all = handed[:, state_dim:]
    chooser = (request_prompt[:, None] == prompt_ids[None, :]).astype(jnp.float32)
    req_states = jnp.einsum("rp,pne->rne", chooser, final_all, precision=lax.Precision.HIGHEST)
    req_edges = jnp.einsum(
        "rp,pje->rje", chooser, edge_all, precision=lax.Precision.HIGHEST
    ).astype(jnp.bfloat16)
    mixed_rows = scatter_rows(
        jnp.dot(gated, w_out, preferred_element_type=jnp.float32).astype(jnp.bfloat16),
        "tp",
        jnp.bfloat16,
    )
    token_rows = lax.dynamic_slice_in_dim(tokens, tp_pos * row_count, row_count, 0)
    residual_rows = token_rows.astype(jnp.float32) + mixed_rows
    normed_rows = rms_norm(residual_rows, mlp_gain).astype(jnp.bfloat16)
    normed_two = gather_rows(normed_rows, "tp")
    gate_val = jnp.dot(normed_two, w_gate, preferred_element_type=jnp.float32)
    up_val = jnp.dot(normed_two, w_up, preferred_element_type=jnp.float32)
    hidden = (jax.nn.silu(gate_val) * up_val).astype(jnp.bfloat16)
    mlp_share = scatter_rows(
        jnp.dot(hidden, w_down, preferred_element_type=jnp.float32).astype(jnp.bfloat16),
        "tp",
        jnp.bfloat16,
    )
    live_rows = lax.dynamic_slice_in_dim(is_live, tp_pos * row_count, row_count, 0).astype(
        jnp.float32
    )
    mixed_out = ((residual_rows + mlp_share) * live_rows[:, None]).astype(jnp.bfloat16)
    return (mixed_out, req_states, req_edges)


def solution(mesh):
    placed = (
        P("seq", None),
        P(),
        P(None, "tp"),
        P(None, "tp"),
        P(None, "tp"),
        P("tp"),
        P("tp", None),
        P(None, "tp"),
        P("tp"),
        P(None, "tp"),
        P("tp"),
        P("tp", None),
        P(),
        P(None, "tp"),
        P(None, "tp"),
        P("tp", None),
        P(),
        P("seq"),
    )
    return jax.shard_map(
        local,
        mesh=mesh,
        in_specs=placed,
        out_specs=(P(("seq", "tp"), None), P("seq", None, "tp"), P("seq", None, "tp")),
        check_vma=False,
    )
```

```python
import functools

import jax
import jax.numpy as jnp
from jax import lax
from jax.experimental import pallas as pl
from jax.experimental.pallas import tpu as pltpu
from jax.sharding import PartitionSpec as P

EPSILON = 1e-05
INTERPRET = False


def from_behind(x, axis, by):
    devices = lax.axis_size(axis)
    pairs = [(i, i + by) for i in range(devices) if 0 <= i + by < devices]
    return lax.ppermute(x, axis, pairs)


def swap(x, axis, bit):
    devices = lax.axis_size(axis)
    return lax.ppermute(x, axis, [(i, i ^ bit) for i in range(devices)])


def bits_of(devices):
    out = []
    bit = 1
    while bit < devices:
        out.append(bit)
        bit *= 2
    assert bit == devices
    return out


def butterfly_sum(x, axis, send_dtype):
    for bit in bits_of(lax.axis_size(axis)):
        x = x + swap(x.astype(send_dtype), axis, bit).astype(x.dtype)
    return x


def scatter_rows(x, axis, first_dtype):
    devices = lax.axis_size(axis)
    bits = bits_of(devices)
    me = lax.axis_index(axis)
    depth = len(bits)
    rows = x.shape[0] // devices
    buf = x.reshape((2,) * depth + (rows, x.shape[1]))
    send_dtype = first_dtype
    for level, bit in enumerate(bits):
        at = depth - 1 - level
        mine = ((me // bit) % 2).astype(jnp.int32)
        keep = lax.dynamic_index_in_dim(buf, mine, at, False)
        give = lax.dynamic_index_in_dim(buf, 1 - mine, at, False)
        got = swap(give.astype(send_dtype), axis, bit)
        buf = keep.astype(jnp.float32) + got.astype(jnp.float32)
    return buf


def gather_rows(x, axis):
    devices = lax.axis_size(axis)
    bits = bits_of(devices)
    me = lax.axis_index(axis)
    buf = x
    for level, bit in enumerate(reversed(bits)):
        got = swap(buf, axis, bit)
        upper = ((me // bit) % 2) == 1
        low = jnp.where(upper, got, buf)
        high = jnp.where(upper, buf, got)
        buf = jnp.stack([low, high], axis=level)
    return buf.reshape((devices * x.shape[0], x.shape[1]))


def rms_norm(values, gain):
    scale = lax.rsqrt(jnp.mean(values * values, axis=-1, keepdims=True) + EPSILON)
    return values * scale * gain


def block_summary_kernel(da_ref, dr_ref, send_ref, atot_ref):
    steps = da_ref.shape[0]

    def chunk(c, carry):
        state, acum = carry
        base = c * 8
        for i in range(8):
            da = da_ref[base + i]
            state = da * state + dr_ref[base + i]
            acum = da * acum
        return state, acum

    zero = jnp.zeros(send_ref.shape, jnp.float32)
    one = jnp.ones(atot_ref.shape, jnp.float32)
    state, acum = lax.fori_loop(0, steps // 8, chunk, (zero, one))
    send_ref[...] = state
    atot_ref[...] = acum


def block_output_kernel(da_ref, dr_ref, om_ref, sin_ref, endf_ref, pid_ref, y_ref, fin_ref):
    steps = da_ref.shape[0]
    width = y_ref.shape[1]
    fin_ref[...] = jnp.zeros(fin_ref.shape, jnp.float32)
    row_ids = lax.broadcasted_iota(jnp.int32, (8, width), 0)

    def chunk(c, state):
        base = pl.multiple_of(c * 8, 8)
        rows = jnp.zeros((8, width), jnp.float32)
        for i in range(8):
            t = base + i
            state = da_ref[t] * state + dr_ref[t]
            here = jnp.sum(om_ref[t] * state, axis=0, keepdims=True)
            rows = jnp.where(row_ids == i, here, rows)

            @pl.when(endf_ref[t] != 0)
            def _():
                fin_ref[pid_ref[t]] = state

        y_ref[pl.ds(base, 8), :] = rows
        return state

    lax.fori_loop(0, steps // 8, chunk, sin_ref[...])


def block_summary(da, dr):
    _, n, e = da.shape
    vmem = pl.BlockSpec(memory_space=pltpu.VMEM)
    return pl.pallas_call(
        block_summary_kernel,
        out_shape=(
            jax.ShapeDtypeStruct((n, e), jnp.float32),
            jax.ShapeDtypeStruct((n, e), jnp.float32),
        ),
        in_specs=[vmem, vmem],
        out_specs=(vmem, vmem),
        interpret=INTERPRET,
    )(da, dr)


def block_output(da, dr, om, sin, endf, pid, prompts):
    t, n, e = da.shape
    vmem = pl.BlockSpec(memory_space=pltpu.VMEM)
    smem = pl.BlockSpec(memory_space=pltpu.SMEM)
    return pl.pallas_call(
        block_output_kernel,
        out_shape=(
            jax.ShapeDtypeStruct((t, e), jnp.float32),
            jax.ShapeDtypeStruct((prompts, n, e), jnp.float32),
        ),
        in_specs=[vmem, vmem, vmem, vmem, smem, smem],
        out_specs=(vmem, vmem),
        interpret=INTERPRET,
    )(da, dr, om, sin, endf, pid)


def entering_state(a_blk, s_blk, axis):
    me = lax.axis_index(axis)
    tot_a, tot_s = a_blk, s_blk
    exc_a, exc_s = jnp.ones_like(a_blk), jnp.zeros_like(s_blk)
    for bit in bits_of(lax.axis_size(axis)):
        got = swap(jnp.stack([tot_a, tot_s]), axis, bit)
        got_a, got_s = got[0], got[1]
        upper = ((me // bit) % 2) == 1
        low_a = jnp.where(upper, got_a, tot_a)
        low_s = jnp.where(upper, got_s, tot_s)
        high_a = jnp.where(upper, tot_a, got_a)
        high_s = jnp.where(upper, tot_s, got_s)
        exc_a, exc_s = (
            jnp.where(upper, got_a * exc_a, exc_a),
            jnp.where(upper, exc_a * got_s + exc_s, exc_s),
        )
        tot_a, tot_s = low_a * high_a, high_a * low_s + high_s
    return exc_s


def local(
    tokens,
    norm_gain,
    w_x,
    w_z,
    conv_w,
    conv_b,
    w_xproj,
    w_dt,
    dt_bias,
    a_log,
    d_skip,
    w_out,
    mlp_gain,
    w_gate,
    w_up,
    w_down,
    prompt_lengths,
    request_prompt,
):
    block_len = tokens.shape[0]
    tp_count = lax.axis_size("tp")
    row_count = block_len // tp_count
    seq_pos = lax.axis_index("seq")
    tp_pos = lax.axis_index("tp")
    first_row = seq_pos * block_len
    prompts = prompt_lengths.shape[0]
    kernel_len = conv_w.shape[0]
    edge_len = kernel_len - 1
    low_dim = w_dt.shape[0]
    state_dim = a_log.shape[0]
    chans = w_x.shape[1]
    places = first_row + jnp.arange(block_len, dtype=jnp.int32)
    prompt_end = jnp.cumsum(prompt_lengths)
    prompt_start = prompt_end - prompt_lengths
    prompt_ids = jnp.arange(prompts, dtype=jnp.int32)
    prompt_of = jnp.sum((places[:, None] >= prompt_end[None, :]).astype(jnp.int32), axis=1)
    start_of = jnp.sum(
        jnp.where(prompt_of[:, None] == prompt_ids[None, :], prompt_start[None, :], 0), axis=1
    )
    offset = places - start_of
    starts_here = jnp.any(places[:, None] == prompt_start[None, :], axis=1)
    ends_here = jnp.any(places[:, None] == prompt_end[None, :] - 1, axis=1)
    is_live = prompt_of < prompts
    seq_count = lax.axis_size("seq")
    behind = lax.ppermute(
        tokens[block_len - edge_len :],
        "seq",
        [(i, (i + 1) % seq_count) for i in range(seq_count)],
    )
    normed = rms_norm(tokens.astype(jnp.float32), norm_gain).astype(jnp.bfloat16)
    normed_behind = rms_norm(behind.astype(jnp.float32), norm_gain).astype(jnp.bfloat16)
    x_branch = jnp.dot(normed, w_x, preferred_element_type=jnp.float32).astype(jnp.bfloat16)
    z_branch = jnp.dot(normed, w_z, preferred_element_type=jnp.float32).astype(jnp.bfloat16)
    x_behind = jnp.dot(normed_behind, w_x, preferred_element_type=jnp.float32).astype(jnp.bfloat16)
    extended = jnp.concatenate([x_behind, x_branch], axis=0)
    conv_sum = jnp.zeros((block_len, chans), jnp.float32) + conv_b[None, :]
    for lag_steps in range(kernel_len):
        window = extended[edge_len - lag_steps : edge_len - lag_steps + block_len].astype(
            jnp.float32
        )
        reach_mask = (offset >= lag_steps).astype(jnp.float32)[:, None]
        conv_sum = conv_sum + conv_w[edge_len - lag_steps][None, :] * window * reach_mask
    conv_out = jax.nn.silu(conv_sum).astype(jnp.bfloat16)
    conv_float = conv_out.astype(jnp.float32)
    projected = butterfly_sum(
        jnp.dot(conv_out, w_xproj, preferred_element_type=jnp.float32), "tp", jnp.float32
    )
    low_rank = projected[:, :low_dim].astype(jnp.bfloat16)
    in_map = projected[:, low_dim : low_dim + state_dim]
    out_map = projected[:, low_dim + state_dim :]
    step_size = jax.nn.softplus(
        jnp.dot(low_rank, w_dt, preferred_element_type=jnp.float32) + dt_bias[None, :]
    )
    decay_rates = -jnp.exp(a_log)
    carry_on = 1.0 - starts_here.astype(jnp.float32)
    decay = jnp.exp(step_size[:, None, :] * decay_rates[None, :, :]) * carry_on[:, None, None]
    drive = (step_size * conv_float)[:, None, :] * in_map[:, :, None]
    out_wide = jnp.broadcast_to(out_map[:, :, None], decay.shape)
    s_blk, a_blk = block_summary(decay, drive)
    state_in = entering_state(a_blk, s_blk, "seq")
    end_flag = ends_here.astype(jnp.int32)
    slot_of = jnp.minimum(prompt_of, prompts - 1).astype(jnp.int32)
    mixer_y, final_part = block_output(decay, drive, out_wide, state_in, end_flag, slot_of, prompts)
    mixer_y = mixer_y + d_skip[None, :] * conv_float
    gated = (mixer_y * jax.nn.silu(z_branch.astype(jnp.float32))).astype(jnp.bfloat16)
    ends_local = (prompt_end - 1 >= first_row) & (prompt_end - 1 < first_row + block_len)
    lag_ids = jnp.arange(edge_len, dtype=jnp.int32)
    ext_rows = jnp.arange(block_len + edge_len, dtype=jnp.int32)
    target_row = prompt_end[:, None] + lag_ids[None, :] - first_row
    inside = (
        prompt_end[:, None] - edge_len + lag_ids[None, :] >= prompt_start[:, None]
    ) & ends_local[:, None]
    edge_pick = ((ext_rows[None, None, :] == target_row[:, :, None]) & inside[:, :, None]).astype(
        jnp.bfloat16
    )
    edge_part = jnp.einsum("pji,ie->pje", edge_pick, extended, preferred_element_type=jnp.float32)
    handed = jnp.concatenate(
        [final_part.astype(jnp.bfloat16), edge_part.astype(jnp.bfloat16)], axis=1
    )
    handed = butterfly_sum(handed, "seq", jnp.bfloat16).astype(jnp.float32)
    final_all = handed[:, :state_dim]
    edge_all = handed[:, state_dim:]
    chooser = (request_prompt[:, None] == prompt_ids[None, :]).astype(jnp.float32)
    req_states = jnp.einsum("rp,pne->rne", chooser, final_all, precision=lax.Precision.HIGHEST)
    req_edges = jnp.einsum(
        "rp,pje->rje", chooser, edge_all, precision=lax.Precision.HIGHEST
    ).astype(jnp.bfloat16)
    mixed_rows = scatter_rows(
        jnp.dot(gated, w_out, preferred_element_type=jnp.float32).astype(jnp.bfloat16),
        "tp",
        jnp.bfloat16,
    )
    token_rows = lax.dynamic_slice_in_dim(tokens, tp_pos * row_count, row_count, 0)
    residual_rows = token_rows.astype(jnp.float32) + mixed_rows
    normed_rows = rms_norm(residual_rows, mlp_gain).astype(jnp.bfloat16)
    normed_two = gather_rows(normed_rows, "tp")
    gate_val = jnp.dot(normed_two, w_gate, preferred_element_type=jnp.float32)
    up_val = jnp.dot(normed_two, w_up, preferred_element_type=jnp.float32)
    hidden = (jax.nn.silu(gate_val) * up_val).astype(jnp.bfloat16)
    mlp_share = scatter_rows(
        jnp.dot(hidden, w_down, preferred_element_type=jnp.float32).astype(jnp.bfloat16),
        "tp",
        jnp.bfloat16,
    )
    live_rows = lax.dynamic_slice_in_dim(is_live, tp_pos * row_count, row_count, 0).astype(
        jnp.float32
    )
    mixed_out = ((residual_rows + mlp_share) * live_rows[:, None]).astype(jnp.bfloat16)
    return (mixed_out, req_states, req_edges)


def solution(mesh):
    placed = (
        P("seq", None),
        P(),
        P(None, "tp"),
        P(None, "tp"),
        P(None, "tp"),
        P("tp"),
        P("tp", None),
        P(None, "tp"),
        P("tp"),
        P(None, "tp"),
        P("tp"),
        P("tp", None),
        P(),
        P(None, "tp"),
        P(None, "tp"),
        P("tp", None),
        P(),
        P("seq"),
    )
    return jax.shard_map(
        local,
        mesh=mesh,
        in_specs=placed,
        out_specs=(P(("seq", "tp"), None), P("seq", None, "tp"), P("seq", None, "tp")),
        check_vma=False,
    )
```

```python
import functools

import jax
import jax.numpy as jnp
from jax import lax
from jax.experimental import pallas as pl
from jax.experimental.pallas import tpu as pltpu
from jax.sharding import PartitionSpec as P

EPSILON = 1e-05
INTERPRET = False


def from_behind(x, axis, by):
    devices = lax.axis_size(axis)
    pairs = [(i, i + by) for i in range(devices) if 0 <= i + by < devices]
    return lax.ppermute(x, axis, pairs)


def swap(x, axis, bit):
    devices = lax.axis_size(axis)
    return lax.ppermute(x, axis, [(i, i ^ bit) for i in range(devices)])


RINGS = {"seq": (8, 4), "tp": (4, 2)}


def ring_vectors(size):
    return {1: [], 2: [1], 4: [1, 3], 8: [1, 2, 6]}[size]


def basis_of(axis):
    devices = lax.axis_size(axis)
    rings = RINGS.get(axis, ())
    prod = 1
    for r in rings:
        prod *= r
    if prod != devices or any(r not in (1, 2, 4, 8) for r in rings):
        rings = (devices,)
    out = []
    shift = 0
    for r in reversed(rings):
        if r > 8:
            vecs = [1 << i for i in range(r.bit_length() - 1)]
            assert 1 << len(vecs) == r
        else:
            vecs = ring_vectors(r)
        for v in vecs:
            out.append((v << shift, (v << shift).bit_length() - 1))
        shift += len(vecs)
    assert 1 << shift == devices
    return out


def butterfly_sum(x, axis, send_dtype):
    for mask, _ in basis_of(axis):
        x = x + swap(x.astype(send_dtype), axis, mask).astype(x.dtype)
    return x


def scatter_order(axis):
    order = sorted(basis_of(axis), key=lambda vh: -vh[1])
    if order[-1] == (1, 0) and all(mask % 2 == 0 for mask, _ in order[:-1]):
        order = order[-1:] + order[:-1]
    return order


def scatter_rows(x, axis, first_dtype):
    devices = lax.axis_size(axis)
    me = lax.axis_index(axis)
    depth = devices.bit_length() - 1
    rows = x.shape[0] // devices
    buf = x.reshape((2,) * depth + (rows, x.shape[1]))
    left = list(range(depth - 1, -1, -1))
    send_dtype = first_dtype
    for mask, top in scatter_order(axis):
        at = left.index(top)
        mine = ((me // (1 << top)) % 2).astype(jnp.int32)
        keep = lax.dynamic_index_in_dim(buf, mine, at, False)
        give = lax.dynamic_index_in_dim(buf, 1 - mine, at, False)
        got = swap(give.astype(send_dtype), axis, mask)
        buf = keep.astype(jnp.float32) + got.astype(jnp.float32)
        left.remove(top)
    return buf


def gather_rows(x, axis):
    devices = lax.axis_size(axis)
    me = lax.axis_index(axis)
    buf = x
    held = []
    for mask, top in reversed(scatter_order(axis)):
        got = swap(buf, axis, mask)
        upper = ((me // (1 << top)) % 2) == 1
        low = jnp.where(upper, got, buf)
        high = jnp.where(upper, buf, got)
        at = sum(1 for b in held if b > top)
        buf = jnp.stack([low, high], axis=at)
        held.insert(at, top)
    return buf.reshape((devices * x.shape[0], x.shape[1]))


def rms_norm(values, gain):
    scale = lax.rsqrt(jnp.mean(values * values, axis=-1, keepdims=True) + EPSILON)
    return values * scale * gain


def block_summary_kernel(da_ref, dr_ref, send_ref, atot_ref):
    steps = da_ref.shape[0]

    def chunk(c, carry):
        state, acum = carry
        base = c * 8
        for i in range(8):
            da = da_ref[base + i]
            state = da * state + dr_ref[base + i]
            acum = da * acum
        return state, acum

    zero = jnp.zeros(send_ref.shape, jnp.float32)
    one = jnp.ones(atot_ref.shape, jnp.float32)
    state, acum = lax.fori_loop(0, steps // 8, chunk, (zero, one))
    send_ref[...] = state
    atot_ref[...] = acum


def block_output_kernel(da_ref, dr_ref, om_ref, sin_ref, endf_ref, pid_ref, y_ref, fin_ref):
    steps = da_ref.shape[0]
    width = y_ref.shape[1]
    fin_ref[...] = jnp.zeros(fin_ref.shape, jnp.float32)
    row_ids = lax.broadcasted_iota(jnp.int32, (8, width), 0)

    def chunk(c, state):
        base = pl.multiple_of(c * 8, 8)
        rows = jnp.zeros((8, width), jnp.float32)
        for i in range(8):
            t = base + i
            state = da_ref[t] * state + dr_ref[t]
            here = jnp.sum(om_ref[t] * state, axis=0, keepdims=True)
            rows = jnp.where(row_ids == i, here, rows)

            @pl.when(endf_ref[t] != 0)
            def _():
                fin_ref[pid_ref[t]] = state

        y_ref[pl.ds(base, 8), :] = rows
        return state

    lax.fori_loop(0, steps // 8, chunk, sin_ref[...])


def block_summary(da, dr):
    _, n, e = da.shape
    vmem = pl.BlockSpec(memory_space=pltpu.VMEM)
    return pl.pallas_call(
        block_summary_kernel,
        out_shape=(
            jax.ShapeDtypeStruct((n, e), jnp.float32),
            jax.ShapeDtypeStruct((n, e), jnp.float32),
        ),
        in_specs=[vmem, vmem],
        out_specs=(vmem, vmem),
        interpret=INTERPRET,
    )(da, dr)


def block_output(da, dr, om, sin, endf, pid, prompts):
    t, n, e = da.shape
    vmem = pl.BlockSpec(memory_space=pltpu.VMEM)
    smem = pl.BlockSpec(memory_space=pltpu.SMEM)
    return pl.pallas_call(
        block_output_kernel,
        out_shape=(
            jax.ShapeDtypeStruct((t, e), jnp.float32),
            jax.ShapeDtypeStruct((prompts, n, e), jnp.float32),
        ),
        in_specs=[vmem, vmem, vmem, vmem, smem, smem],
        out_specs=(vmem, vmem),
        interpret=INTERPRET,
    )(da, dr, om, sin, endf, pid)


def entering_state(a_blk, s_blk, axis):
    me = lax.axis_index(axis)
    tot_a, tot_s = a_blk, s_blk
    exc_a, exc_s = jnp.ones_like(a_blk), jnp.zeros_like(s_blk)
    for mask, top in basis_of(axis):
        got = swap(jnp.stack([tot_a, tot_s]), axis, mask)
        got_a, got_s = got[0], got[1]
        upper = ((me // (1 << top)) % 2) == 1
        low_a = jnp.where(upper, got_a, tot_a)
        low_s = jnp.where(upper, got_s, tot_s)
        high_a = jnp.where(upper, tot_a, got_a)
        high_s = jnp.where(upper, tot_s, got_s)
        exc_a, exc_s = (
            jnp.where(upper, got_a * exc_a, exc_a),
            jnp.where(upper, exc_a * got_s + exc_s, exc_s),
        )
        tot_a, tot_s = low_a * high_a, high_a * low_s + high_s
    return exc_s


def local(
    tokens,
    norm_gain,
    w_x,
    w_z,
    conv_w,
    conv_b,
    w_xproj,
    w_dt,
    dt_bias,
    a_log,
    d_skip,
    w_out,
    mlp_gain,
    w_gate,
    w_up,
    w_down,
    prompt_lengths,
    request_prompt,
):
    block_len = tokens.shape[0]
    tp_count = lax.axis_size("tp")
    row_count = block_len // tp_count
    seq_pos = lax.axis_index("seq")
    tp_pos = lax.axis_index("tp")
    first_row = seq_pos * block_len
    prompts = prompt_lengths.shape[0]
    kernel_len = conv_w.shape[0]
    edge_len = kernel_len - 1
    low_dim = w_dt.shape[0]
    state_dim = a_log.shape[0]
    chans = w_x.shape[1]
    places = first_row + jnp.arange(block_len, dtype=jnp.int32)
    prompt_end = jnp.cumsum(prompt_lengths)
    prompt_start = prompt_end - prompt_lengths
    prompt_ids = jnp.arange(prompts, dtype=jnp.int32)
    prompt_of = jnp.sum((places[:, None] >= prompt_end[None, :]).astype(jnp.int32), axis=1)
    start_of = jnp.sum(
        jnp.where(prompt_of[:, None] == prompt_ids[None, :], prompt_start[None, :], 0), axis=1
    )
    offset = places - start_of
    starts_here = jnp.any(places[:, None] == prompt_start[None, :], axis=1)
    ends_here = jnp.any(places[:, None] == prompt_end[None, :] - 1, axis=1)
    is_live = prompt_of < prompts
    seq_count = lax.axis_size("seq")
    behind = lax.ppermute(
        tokens[block_len - edge_len :],
        "seq",
        [(i, (i + 1) % seq_count) for i in range(seq_count)],
    )
    normed = rms_norm(tokens.astype(jnp.float32), norm_gain).astype(jnp.bfloat16)
    normed_behind = rms_norm(behind.astype(jnp.float32), norm_gain).astype(jnp.bfloat16)
    x_branch = jnp.dot(normed, w_x, preferred_element_type=jnp.float32).astype(jnp.bfloat16)
    z_branch = jnp.dot(normed, w_z, preferred_element_type=jnp.float32).astype(jnp.bfloat16)
    x_behind = jnp.dot(normed_behind, w_x, preferred_element_type=jnp.float32).astype(jnp.bfloat16)
    extended = jnp.concatenate([x_behind, x_branch], axis=0)
    conv_sum = jnp.zeros((block_len, chans), jnp.float32) + conv_b[None, :]
    for lag_steps in range(kernel_len):
        window = extended[edge_len - lag_steps : edge_len - lag_steps + block_len].astype(
            jnp.float32
        )
        reach_mask = (offset >= lag_steps).astype(jnp.float32)[:, None]
        conv_sum = conv_sum + conv_w[edge_len - lag_steps][None, :] * window * reach_mask
    conv_out = jax.nn.silu(conv_sum).astype(jnp.bfloat16)
    conv_float = conv_out.astype(jnp.float32)
    projected = butterfly_sum(
        jnp.dot(conv_out, w_xproj, preferred_element_type=jnp.float32), "tp", jnp.float32
    )
    low_rank = projected[:, :low_dim].astype(jnp.bfloat16)
    in_map = projected[:, low_dim : low_dim + state_dim]
    out_map = projected[:, low_dim + state_dim :]
    step_size = jax.nn.softplus(
        jnp.dot(low_rank, w_dt, preferred_element_type=jnp.float32) + dt_bias[None, :]
    )
    decay_rates = -jnp.exp(a_log)
    carry_on = 1.0 - starts_here.astype(jnp.float32)
    decay = jnp.exp(step_size[:, None, :] * decay_rates[None, :, :]) * carry_on[:, None, None]
    drive = (step_size * conv_float)[:, None, :] * in_map[:, :, None]
    out_wide = jnp.broadcast_to(out_map[:, :, None], decay.shape)
    s_blk, a_blk = block_summary(decay, drive)
    state_in = entering_state(a_blk, s_blk, "seq")
    end_flag = ends_here.astype(jnp.int32)
    slot_of = jnp.minimum(prompt_of, prompts - 1).astype(jnp.int32)
    mixer_y, final_part = block_output(decay, drive, out_wide, state_in, end_flag, slot_of, prompts)
    mixer_y = mixer_y + d_skip[None, :] * conv_float
    gated = (mixer_y * jax.nn.silu(z_branch.astype(jnp.float32))).astype(jnp.bfloat16)
    ends_local = (prompt_end - 1 >= first_row) & (prompt_end - 1 < first_row + block_len)
    lag_ids = jnp.arange(edge_len, dtype=jnp.int32)
    ext_rows = jnp.arange(block_len + edge_len, dtype=jnp.int32)
    target_row = prompt_end[:, None] + lag_ids[None, :] - first_row
    inside = (
        prompt_end[:, None] - edge_len + lag_ids[None, :] >= prompt_start[:, None]
    ) & ends_local[:, None]
    edge_pick = ((ext_rows[None, None, :] == target_row[:, :, None]) & inside[:, :, None]).astype(
        jnp.bfloat16
    )
    edge_part = jnp.einsum("pji,ie->pje", edge_pick, extended, preferred_element_type=jnp.float32)
    handed = jnp.concatenate(
        [final_part.astype(jnp.bfloat16), edge_part.astype(jnp.bfloat16)], axis=1
    )
    handed = butterfly_sum(handed, "seq", jnp.bfloat16).astype(jnp.float32)
    final_all = handed[:, :state_dim]
    edge_all = handed[:, state_dim:]
    chooser = (request_prompt[:, None] == prompt_ids[None, :]).astype(jnp.float32)
    req_states = jnp.einsum("rp,pne->rne", chooser, final_all, precision=lax.Precision.HIGHEST)
    req_edges = jnp.einsum(
        "rp,pje->rje", chooser, edge_all, precision=lax.Precision.HIGHEST
    ).astype(jnp.bfloat16)
    mixed_rows = scatter_rows(
        jnp.dot(gated, w_out, preferred_element_type=jnp.float32).astype(jnp.bfloat16),
        "tp",
        jnp.bfloat16,
    )
    token_rows = lax.dynamic_slice_in_dim(tokens, tp_pos * row_count, row_count, 0)
    residual_rows = token_rows.astype(jnp.float32) + mixed_rows
    normed_rows = rms_norm(residual_rows, mlp_gain).astype(jnp.bfloat16)
    normed_two = gather_rows(normed_rows, "tp")
    gate_val = jnp.dot(normed_two, w_gate, preferred_element_type=jnp.float32)
    up_val = jnp.dot(normed_two, w_up, preferred_element_type=jnp.float32)
    hidden = (jax.nn.silu(gate_val) * up_val).astype(jnp.bfloat16)
    mlp_share = scatter_rows(
        jnp.dot(hidden, w_down, preferred_element_type=jnp.float32).astype(jnp.bfloat16),
        "tp",
        jnp.bfloat16,
    )
    live_rows = lax.dynamic_slice_in_dim(is_live, tp_pos * row_count, row_count, 0).astype(
        jnp.float32
    )
    mixed_out = ((residual_rows + mlp_share) * live_rows[:, None]).astype(jnp.bfloat16)
    return (mixed_out, req_states, req_edges)


def solution(mesh):
    placed = (
        P("seq", None),
        P(),
        P(None, "tp"),
        P(None, "tp"),
        P(None, "tp"),
        P("tp"),
        P("tp", None),
        P(None, "tp"),
        P("tp"),
        P(None, "tp"),
        P("tp"),
        P("tp", None),
        P(),
        P(None, "tp"),
        P(None, "tp"),
        P("tp", None),
        P(),
        P("seq"),
    )
    return jax.shard_map(
        local,
        mesh=mesh,
        in_specs=placed,
        out_specs=(P(("seq", "tp"), None), P("seq", None, "tp"), P("seq", None, "tp")),
        check_vma=False,
    )
```

```python
import functools

import jax
import jax.numpy as jnp
from jax import lax
from jax.experimental import pallas as pl
from jax.experimental.pallas import tpu as pltpu
from jax.sharding import PartitionSpec as P

EPSILON = 1e-05
INTERPRET = False


def from_behind(x, axis, by):
    devices = lax.axis_size(axis)
    pairs = [(i, i + by) for i in range(devices) if 0 <= i + by < devices]
    return lax.ppermute(x, axis, pairs)


def swap(x, axis, bit):
    devices = lax.axis_size(axis)
    return lax.ppermute(x, axis, [(i, i ^ bit) for i in range(devices)])


RINGS = {"seq": (8, 4), "tp": (4, 2)}


def ring_vectors(size):
    return {1: [], 2: [1], 4: [1, 3], 8: [1, 2, 6]}[size]


def basis_of(axis):
    devices = lax.axis_size(axis)
    rings = RINGS.get(axis, ())
    prod = 1
    for r in rings:
        prod *= r
    if prod != devices or any(r not in (1, 2, 4, 8) for r in rings):
        rings = (devices,)
    out = []
    shift = 0
    for r in reversed(rings):
        if r > 8:
            vecs = [1 << i for i in range(r.bit_length() - 1)]
            assert 1 << len(vecs) == r
        else:
            vecs = ring_vectors(r)
        for v in vecs:
            out.append((v << shift, (v << shift).bit_length() - 1))
        shift += len(vecs)
    assert 1 << shift == devices
    return out


def butterfly_sum(x, axis, send_dtype):
    for mask, _ in basis_of(axis):
        x = x + swap(x.astype(send_dtype), axis, mask).astype(x.dtype)
    return x


def scatter_order(axis):
    order = sorted(basis_of(axis), key=lambda vh: -vh[1])
    if order[-1] == (1, 0) and all(mask % 2 == 0 for mask, _ in order[:-1]):
        order = order[-1:] + order[:-1]
    return order


def scatter_rows(x, axis, first_dtype):
    devices = lax.axis_size(axis)
    me = lax.axis_index(axis)
    depth = devices.bit_length() - 1
    rows = x.shape[0] // devices
    buf = x.reshape((2,) * depth + (rows, x.shape[1]))
    left = list(range(depth - 1, -1, -1))
    send_dtype = first_dtype
    for mask, top in scatter_order(axis):
        at = left.index(top)
        mine = ((me // (1 << top)) % 2).astype(jnp.int32)
        keep = lax.dynamic_index_in_dim(buf, mine, at, False)
        give = lax.dynamic_index_in_dim(buf, 1 - mine, at, False)
        got = swap(give.astype(send_dtype), axis, mask)
        buf = keep.astype(jnp.float32) + got.astype(jnp.float32)
        left.remove(top)
    return buf


def gather_rows(x, axis):
    devices = lax.axis_size(axis)
    me = lax.axis_index(axis)
    buf = x
    held = []
    for mask, top in reversed(scatter_order(axis)):
        got = swap(buf, axis, mask)
        upper = ((me // (1 << top)) % 2) == 1
        low = jnp.where(upper, got, buf)
        high = jnp.where(upper, buf, got)
        at = sum(1 for b in held if b > top)
        buf = jnp.stack([low, high], axis=at)
        held.insert(at, top)
    return buf.reshape((devices * x.shape[0], x.shape[1]))


def fin_round(buf, mask, tie):
    got = swap(buf, "seq", mask)
    got, tie = lax.optimization_barrier((got, tie))
    return buf + got, tie


def rms_norm(values, gain):
    scale = lax.rsqrt(jnp.mean(values * values, axis=-1, keepdims=True) + EPSILON)
    return values * scale * gain


def block_summary_kernel(da_ref, dr_ref, endf_ref, pid_ref, send_ref, atot_ref, fs_ref, fd_ref):
    steps = da_ref.shape[0]
    fs_ref[...] = jnp.zeros(fs_ref.shape, jnp.float32)
    fd_ref[...] = jnp.zeros(fd_ref.shape, jnp.float32)

    def chunk(c, carry):
        state, acum = carry
        base = c * 8
        for i in range(8):
            t = base + i
            da = da_ref[t]
            state = da * state + dr_ref[t]
            acum = da * acum

            @pl.when(endf_ref[t] != 0)
            def _():
                fs_ref[pid_ref[t]] = state
                fd_ref[pid_ref[t]] = acum

        return state, acum

    zero = jnp.zeros(send_ref.shape, jnp.float32)
    one = jnp.ones(atot_ref.shape, jnp.float32)
    state, acum = lax.fori_loop(0, steps // 8, chunk, (zero, one))
    send_ref[...] = state
    atot_ref[...] = acum


def block_output_kernel(da_ref, dr_ref, om_ref, sin_ref, y_ref):
    steps = da_ref.shape[0]
    width = y_ref.shape[1]
    row_ids = lax.broadcasted_iota(jnp.int32, (8, width), 0)

    def chunk(c, state):
        base = pl.multiple_of(c * 8, 8)
        rows = jnp.zeros((8, width), jnp.float32)
        for i in range(8):
            t = base + i
            state = da_ref[t] * state + dr_ref[t]
            here = jnp.sum(om_ref[t] * state, axis=0, keepdims=True)
            rows = jnp.where(row_ids == i, here, rows)
        y_ref[pl.ds(base, 8), :] = rows
        return state

    lax.fori_loop(0, steps // 8, chunk, sin_ref[...])


def block_summary(da, dr, endf, pid, prompts):
    _, n, e = da.shape
    vmem = pl.BlockSpec(memory_space=pltpu.VMEM)
    smem = pl.BlockSpec(memory_space=pltpu.SMEM)
    return pl.pallas_call(
        block_summary_kernel,
        out_shape=(
            jax.ShapeDtypeStruct((n, e), jnp.float32),
            jax.ShapeDtypeStruct((n, e), jnp.float32),
            jax.ShapeDtypeStruct((prompts, n, e), jnp.float32),
            jax.ShapeDtypeStruct((prompts, n, e), jnp.float32),
        ),
        in_specs=[vmem, vmem, smem, smem],
        out_specs=(vmem, vmem, vmem, vmem),
        interpret=INTERPRET,
    )(da, dr, endf, pid)


def block_output(da, dr, om, sin):
    t, n, e = da.shape
    vmem = pl.BlockSpec(memory_space=pltpu.VMEM)
    return pl.pallas_call(
        block_output_kernel,
        out_shape=jax.ShapeDtypeStruct((t, e), jnp.float32),
        in_specs=[vmem, vmem, vmem, vmem],
        out_specs=vmem,
        interpret=INTERPRET,
    )(da, dr, om, sin)


def entering_state(a_blk, s_blk, axis):
    me = lax.axis_index(axis)
    tot_a, tot_s = a_blk, s_blk
    exc_a, exc_s = jnp.ones_like(a_blk), jnp.zeros_like(s_blk)
    for mask, top in basis_of(axis):
        got = swap(jnp.stack([tot_a, tot_s]), axis, mask)
        got_a, got_s = got[0], got[1]
        upper = ((me // (1 << top)) % 2) == 1
        low_a = jnp.where(upper, got_a, tot_a)
        low_s = jnp.where(upper, got_s, tot_s)
        high_a = jnp.where(upper, tot_a, got_a)
        high_s = jnp.where(upper, tot_s, got_s)
        exc_a, exc_s = (
            jnp.where(upper, got_a * exc_a, exc_a),
            jnp.where(upper, exc_a * got_s + exc_s, exc_s),
        )
        tot_a, tot_s = low_a * high_a, high_a * low_s + high_s
    return exc_s


def local(
    tokens,
    norm_gain,
    w_x,
    w_z,
    conv_w,
    conv_b,
    w_xproj,
    w_dt,
    dt_bias,
    a_log,
    d_skip,
    w_out,
    mlp_gain,
    w_gate,
    w_up,
    w_down,
    prompt_lengths,
    request_prompt,
):
    block_len = tokens.shape[0]
    tp_count = lax.axis_size("tp")
    row_count = block_len // tp_count
    seq_pos = lax.axis_index("seq")
    tp_pos = lax.axis_index("tp")
    first_row = seq_pos * block_len
    prompts = prompt_lengths.shape[0]
    kernel_len = conv_w.shape[0]
    edge_len = kernel_len - 1
    low_dim = w_dt.shape[0]
    state_dim = a_log.shape[0]
    chans = w_x.shape[1]
    places = first_row + jnp.arange(block_len, dtype=jnp.int32)
    prompt_end = jnp.cumsum(prompt_lengths)
    prompt_start = prompt_end - prompt_lengths
    prompt_ids = jnp.arange(prompts, dtype=jnp.int32)
    prompt_of = jnp.sum((places[:, None] >= prompt_end[None, :]).astype(jnp.int32), axis=1)
    start_of = jnp.sum(
        jnp.where(prompt_of[:, None] == prompt_ids[None, :], prompt_start[None, :], 0), axis=1
    )
    offset = places - start_of
    starts_here = jnp.any(places[:, None] == prompt_start[None, :], axis=1)
    ends_here = jnp.any(places[:, None] == prompt_end[None, :] - 1, axis=1)
    is_live = prompt_of < prompts
    seq_count = lax.axis_size("seq")
    behind = lax.ppermute(
        tokens[block_len - edge_len :],
        "seq",
        [(i, (i + 1) % seq_count) for i in range(seq_count)],
    )
    normed = rms_norm(tokens.astype(jnp.float32), norm_gain).astype(jnp.bfloat16)
    normed_behind = rms_norm(behind.astype(jnp.float32), norm_gain).astype(jnp.bfloat16)
    x_branch = jnp.dot(normed, w_x, preferred_element_type=jnp.float32).astype(jnp.bfloat16)
    z_branch = jnp.dot(normed, w_z, preferred_element_type=jnp.float32).astype(jnp.bfloat16)
    x_behind = jnp.dot(normed_behind, w_x, preferred_element_type=jnp.float32).astype(jnp.bfloat16)
    extended = jnp.concatenate([x_behind, x_branch], axis=0)
    conv_sum = jnp.zeros((block_len, chans), jnp.float32) + conv_b[None, :]
    for lag_steps in range(kernel_len):
        window = extended[edge_len - lag_steps : edge_len - lag_steps + block_len].astype(
            jnp.float32
        )
        reach_mask = (offset >= lag_steps).astype(jnp.float32)[:, None]
        conv_sum = conv_sum + conv_w[edge_len - lag_steps][None, :] * window * reach_mask
    conv_out = jax.nn.silu(conv_sum).astype(jnp.bfloat16)
    conv_float = conv_out.astype(jnp.float32)
    projected = butterfly_sum(
        jnp.dot(conv_out, w_xproj, preferred_element_type=jnp.float32), "tp", jnp.float32
    )
    low_rank = projected[:, :low_dim].astype(jnp.bfloat16)
    in_map = projected[:, low_dim : low_dim + state_dim]
    out_map = projected[:, low_dim + state_dim :]
    step_size = jax.nn.softplus(
        jnp.dot(low_rank, w_dt, preferred_element_type=jnp.float32) + dt_bias[None, :]
    )
    decay_rates = -jnp.exp(a_log)
    carry_on = 1.0 - starts_here.astype(jnp.float32)
    decay = jnp.exp(step_size[:, None, :] * decay_rates[None, :, :]) * carry_on[:, None, None]
    drive = (step_size * conv_float)[:, None, :] * in_map[:, :, None]
    out_wide = jnp.broadcast_to(out_map[:, :, None], decay.shape)
    end_flag = ends_here.astype(jnp.int32)
    slot_of = jnp.minimum(prompt_of, prompts - 1).astype(jnp.int32)
    s_blk, a_blk, end_state, end_decay = block_summary(decay, drive, end_flag, slot_of, prompts)
    state_in = entering_state(a_blk, s_blk, "seq")
    final_part = end_state + end_decay * state_in[None]
    mixer_y = block_output(decay, drive, out_wide, state_in)
    fin_masks = [mask for mask, _ in basis_of("seq")]
    ends_local = (prompt_end - 1 >= first_row) & (prompt_end - 1 < first_row + block_len)
    lag_ids = jnp.arange(edge_len, dtype=jnp.int32)
    ext_rows = jnp.arange(block_len + edge_len, dtype=jnp.int32)
    target_row = prompt_end[:, None] + lag_ids[None, :] - first_row
    inside = (
        prompt_end[:, None] - edge_len + lag_ids[None, :] >= prompt_start[:, None]
    ) & ends_local[:, None]
    edge_pick = ((ext_rows[None, None, :] == target_row[:, :, None]) & inside[:, :, None]).astype(
        jnp.bfloat16
    )
    edge_part = jnp.einsum("pji,ie->pje", edge_pick, extended, preferred_element_type=jnp.float32)
    handed = jnp.concatenate(
        [final_part.astype(jnp.bfloat16), edge_part.astype(jnp.bfloat16)], axis=1
    )
    handed, mixer_y = fin_round(handed, fin_masks[0], mixer_y)
    mixer_y = mixer_y + d_skip[None, :] * conv_float
    gated = (mixer_y * jax.nn.silu(z_branch.astype(jnp.float32))).astype(jnp.bfloat16)
    mixed_part = jnp.dot(gated, w_out, preferred_element_type=jnp.float32).astype(jnp.bfloat16)
    handed, mixed_part = fin_round(handed, fin_masks[1], mixed_part)
    mixed_rows = scatter_rows(mixed_part, "tp", jnp.bfloat16)
    handed, mixed_rows = fin_round(handed, fin_masks[2], mixed_rows)
    token_rows = lax.dynamic_slice_in_dim(tokens, tp_pos * row_count, row_count, 0)
    residual_rows = token_rows.astype(jnp.float32) + mixed_rows
    normed_rows = rms_norm(residual_rows, mlp_gain).astype(jnp.bfloat16)
    normed_two = gather_rows(normed_rows, "tp")
    handed, normed_two = fin_round(handed, fin_masks[3], normed_two)
    gate_val = jnp.dot(normed_two, w_gate, preferred_element_type=jnp.float32)
    up_val = jnp.dot(normed_two, w_up, preferred_element_type=jnp.float32)
    hidden = (jax.nn.silu(gate_val) * up_val).astype(jnp.bfloat16)
    mlp_part = jnp.dot(hidden, w_down, preferred_element_type=jnp.float32).astype(jnp.bfloat16)
    handed, mlp_part = fin_round(handed, fin_masks[4], mlp_part)
    for mask in fin_masks[5:]:
        handed = handed + swap(handed, "seq", mask)
    handed = handed.astype(jnp.float32)
    mlp_share = scatter_rows(mlp_part, "tp", jnp.bfloat16)
    final_all = handed[:, :state_dim]
    edge_all = handed[:, state_dim:]
    chooser = (request_prompt[:, None] == prompt_ids[None, :]).astype(jnp.float32)
    req_states = jnp.einsum("rp,pne->rne", chooser, final_all, precision=lax.Precision.HIGHEST)
    req_edges = jnp.einsum(
        "rp,pje->rje", chooser, edge_all, precision=lax.Precision.HIGHEST
    ).astype(jnp.bfloat16)
    live_rows = lax.dynamic_slice_in_dim(is_live, tp_pos * row_count, row_count, 0).astype(
        jnp.float32
    )
    mixed_out = ((residual_rows + mlp_share) * live_rows[:, None]).astype(jnp.bfloat16)
    return (mixed_out, req_states, req_edges)


def solution(mesh):
    placed = (
        P("seq", None),
        P(),
        P(None, "tp"),
        P(None, "tp"),
        P(None, "tp"),
        P("tp"),
        P("tp", None),
        P(None, "tp"),
        P("tp"),
        P(None, "tp"),
        P("tp"),
        P("tp", None),
        P(),
        P(None, "tp"),
        P(None, "tp"),
        P("tp", None),
        P(),
        P("seq"),
    )
    return jax.shard_map(
        local,
        mesh=mesh,
        in_specs=placed,
        out_specs=(P(("seq", "tp"), None), P("seq", None, "tp"), P("seq", None, "tp")),
        check_vma=False,
    )
```

```python
import functools

import jax
import jax.numpy as jnp
from jax import lax
from jax.experimental import pallas as pl
from jax.experimental.pallas import tpu as pltpu
from jax.sharding import PartitionSpec as P

EPSILON = 1e-05
INTERPRET = False


def from_behind(x, axis, by):
    devices = lax.axis_size(axis)
    pairs = [(i, i + by) for i in range(devices) if 0 <= i + by < devices]
    return lax.ppermute(x, axis, pairs)


def swap(x, axis, bit):
    devices = lax.axis_size(axis)
    return lax.ppermute(x, axis, [(i, i ^ bit) for i in range(devices)])


RINGS = {"seq": (8, 4), "tp": (4, 2)}


def ring_vectors(size):
    return {1: [], 2: [1], 4: [1, 3], 8: [1, 2, 6]}[size]


def basis_of(axis):
    devices = lax.axis_size(axis)
    rings = RINGS.get(axis, ())
    prod = 1
    for r in rings:
        prod *= r
    if prod != devices or any(r not in (1, 2, 4, 8) for r in rings):
        rings = (devices,)
    out = []
    shift = 0
    for r in reversed(rings):
        if r > 8:
            vecs = [1 << i for i in range(r.bit_length() - 1)]
            assert 1 << len(vecs) == r
        else:
            vecs = ring_vectors(r)
        for v in vecs:
            out.append((v << shift, (v << shift).bit_length() - 1))
        shift += len(vecs)
    assert 1 << shift == devices
    return out


def butterfly_sum(x, axis, send_dtype):
    for mask, _ in basis_of(axis):
        x = x + swap(x.astype(send_dtype), axis, mask).astype(x.dtype)
    return x


def scatter_order(axis):
    order = sorted(basis_of(axis), key=lambda vh: -vh[1])
    if order[-1] == (1, 0) and all(mask % 2 == 0 for mask, _ in order[:-1]):
        order = order[-1:] + order[:-1]
    return order


def scatter_rows(x, axis, first_dtype):
    devices = lax.axis_size(axis)
    me = lax.axis_index(axis)
    depth = devices.bit_length() - 1
    rows = x.shape[0] // devices
    buf = x.reshape((2,) * depth + (rows, x.shape[1]))
    left = list(range(depth - 1, -1, -1))
    send_dtype = first_dtype
    for mask, top in scatter_order(axis):
        at = left.index(top)
        mine = ((me // (1 << top)) % 2).astype(jnp.int32)
        keep = lax.dynamic_index_in_dim(buf, mine, at, False)
        give = lax.dynamic_index_in_dim(buf, 1 - mine, at, False)
        got = swap(give.astype(send_dtype), axis, mask)
        buf = keep.astype(jnp.float32) + got.astype(jnp.float32)
        left.remove(top)
    return buf


def gather_rows(x, axis):
    devices = lax.axis_size(axis)
    me = lax.axis_index(axis)
    buf = x
    held = []
    for mask, top in reversed(scatter_order(axis)):
        got = swap(buf, axis, mask)
        upper = ((me // (1 << top)) % 2) == 1
        low = jnp.where(upper, got, buf)
        high = jnp.where(upper, buf, got)
        at = sum(1 for b in held if b > top)
        buf = jnp.stack([low, high], axis=at)
        held.insert(at, top)
    return buf.reshape((devices * x.shape[0], x.shape[1]))


def rms_norm(values, gain):
    scale = lax.rsqrt(jnp.mean(values * values, axis=-1, keepdims=True) + EPSILON)
    return values * scale * gain


def block_summary_kernel(da_ref, dr_ref, send_ref, atot_ref):
    steps = da_ref.shape[0]
    half = steps // 2

    def chunk(c, carry):
        s1, a1, s2, a2 = carry
        base = c * 8
        for i in range(8):
            d1 = da_ref[base + i]
            d2 = da_ref[half + base + i]
            s1 = d1 * s1 + dr_ref[base + i]
            s2 = d2 * s2 + dr_ref[half + base + i]
            a1 = d1 * a1
            a2 = d2 * a2
        return s1, a1, s2, a2

    zero = jnp.zeros(send_ref.shape, jnp.float32)
    one = jnp.ones(atot_ref.shape, jnp.float32)
    s1, a1, s2, a2 = lax.fori_loop(0, half // 8, chunk, (zero, one, zero, one))
    send_ref[...] = a2 * s1 + s2
    atot_ref[...] = a1 * a2


def block_output_kernel(da_ref, dr_ref, om_ref, sin_ref, endf_ref, pid_ref, y_ref, fin_ref):
    steps = da_ref.shape[0]
    width = y_ref.shape[1]
    fin_ref[...] = jnp.zeros(fin_ref.shape, jnp.float32)
    row_ids = lax.broadcasted_iota(jnp.int32, (8, width), 0)

    def chunk(c, state):
        base = pl.multiple_of(c * 8, 8)
        rows = jnp.zeros((8, width), jnp.float32)
        for i in range(8):
            t = base + i
            state = da_ref[t] * state + dr_ref[t]
            here = jnp.sum(om_ref[t] * state, axis=0, keepdims=True)
            rows = jnp.where(row_ids == i, here, rows)

            @pl.when(endf_ref[t] != 0)
            def _():
                fin_ref[pid_ref[t]] = state

        y_ref[pl.ds(base, 8), :] = rows
        return state

    lax.fori_loop(0, steps // 8, chunk, sin_ref[...])


def block_summary(da, dr):
    _, n, e = da.shape
    vmem = pl.BlockSpec(memory_space=pltpu.VMEM)
    return pl.pallas_call(
        block_summary_kernel,
        out_shape=(
            jax.ShapeDtypeStruct((n, e), jnp.float32),
            jax.ShapeDtypeStruct((n, e), jnp.float32),
        ),
        in_specs=[vmem, vmem],
        out_specs=(vmem, vmem),
        interpret=INTERPRET,
    )(da, dr)


def block_output(da, dr, om, sin, endf, pid, prompts):
    t, n, e = da.shape
    vmem = pl.BlockSpec(memory_space=pltpu.VMEM)
    smem = pl.BlockSpec(memory_space=pltpu.SMEM)
    return pl.pallas_call(
        block_output_kernel,
        out_shape=(
            jax.ShapeDtypeStruct((t, e), jnp.float32),
            jax.ShapeDtypeStruct((prompts, n, e), jnp.float32),
        ),
        in_specs=[vmem, vmem, vmem, vmem, smem, smem],
        out_specs=(vmem, vmem),
        interpret=INTERPRET,
    )(da, dr, om, sin, endf, pid)


def entering_state(a_blk, s_blk, axis):
    me = lax.axis_index(axis)
    tot_a, tot_s = a_blk, s_blk
    exc_a, exc_s = jnp.ones_like(a_blk), jnp.zeros_like(s_blk)
    for mask, top in basis_of(axis):
        got = swap(jnp.stack([tot_a, tot_s]), axis, mask)
        got_a, got_s = got[0], got[1]
        upper = ((me // (1 << top)) % 2) == 1
        low_a = jnp.where(upper, got_a, tot_a)
        low_s = jnp.where(upper, got_s, tot_s)
        high_a = jnp.where(upper, tot_a, got_a)
        high_s = jnp.where(upper, tot_s, got_s)
        exc_a, exc_s = (
            jnp.where(upper, got_a * exc_a, exc_a),
            jnp.where(upper, exc_a * got_s + exc_s, exc_s),
        )
        tot_a, tot_s = low_a * high_a, high_a * low_s + high_s
    return exc_s


def local(
    tokens,
    norm_gain,
    w_x,
    w_z,
    conv_w,
    conv_b,
    w_xproj,
    w_dt,
    dt_bias,
    a_log,
    d_skip,
    w_out,
    mlp_gain,
    w_gate,
    w_up,
    w_down,
    prompt_lengths,
    request_prompt,
):
    block_len = tokens.shape[0]
    tp_count = lax.axis_size("tp")
    row_count = block_len // tp_count
    seq_pos = lax.axis_index("seq")
    tp_pos = lax.axis_index("tp")
    first_row = seq_pos * block_len
    prompts = prompt_lengths.shape[0]
    kernel_len = conv_w.shape[0]
    edge_len = kernel_len - 1
    low_dim = w_dt.shape[0]
    state_dim = a_log.shape[0]
    chans = w_x.shape[1]
    places = first_row + jnp.arange(block_len, dtype=jnp.int32)
    prompt_end = jnp.cumsum(prompt_lengths)
    prompt_start = prompt_end - prompt_lengths
    prompt_ids = jnp.arange(prompts, dtype=jnp.int32)
    prompt_of = jnp.sum((places[:, None] >= prompt_end[None, :]).astype(jnp.int32), axis=1)
    start_of = jnp.sum(
        jnp.where(prompt_of[:, None] == prompt_ids[None, :], prompt_start[None, :], 0), axis=1
    )
    offset = places - start_of
    starts_here = jnp.any(places[:, None] == prompt_start[None, :], axis=1)
    ends_here = jnp.any(places[:, None] == prompt_end[None, :] - 1, axis=1)
    is_live = prompt_of < prompts
    seq_count = lax.axis_size("seq")
    behind = lax.ppermute(
        tokens[block_len - edge_len :],
        "seq",
        [(i, (i + 1) % seq_count) for i in range(seq_count)],
    )
    normed = rms_norm(tokens.astype(jnp.float32), norm_gain).astype(jnp.bfloat16)
    normed_behind = rms_norm(behind.astype(jnp.float32), norm_gain).astype(jnp.bfloat16)
    x_branch = jnp.dot(normed, w_x, preferred_element_type=jnp.float32).astype(jnp.bfloat16)
    z_branch = jnp.dot(normed, w_z, preferred_element_type=jnp.float32).astype(jnp.bfloat16)
    x_behind = jnp.dot(normed_behind, w_x, preferred_element_type=jnp.float32).astype(jnp.bfloat16)
    extended = jnp.concatenate([x_behind, x_branch], axis=0)
    conv_sum = jnp.zeros((block_len, chans), jnp.float32) + conv_b[None, :]
    for lag_steps in range(kernel_len):
        window = extended[edge_len - lag_steps : edge_len - lag_steps + block_len].astype(
            jnp.float32
        )
        reach_mask = (offset >= lag_steps).astype(jnp.float32)[:, None]
        conv_sum = conv_sum + conv_w[edge_len - lag_steps][None, :] * window * reach_mask
    conv_out = jax.nn.silu(conv_sum).astype(jnp.bfloat16)
    conv_float = conv_out.astype(jnp.float32)
    projected = butterfly_sum(
        jnp.dot(conv_out, w_xproj, preferred_element_type=jnp.float32), "tp", jnp.float32
    )
    low_rank = projected[:, :low_dim].astype(jnp.bfloat16)
    in_map = projected[:, low_dim : low_dim + state_dim]
    out_map = projected[:, low_dim + state_dim :]
    step_size = jax.nn.softplus(
        jnp.dot(low_rank, w_dt, preferred_element_type=jnp.float32) + dt_bias[None, :]
    )
    decay_rates = -jnp.exp(a_log)
    carry_on = 1.0 - starts_here.astype(jnp.float32)
    decay = jnp.exp(step_size[:, None, :] * decay_rates[None, :, :]) * carry_on[:, None, None]
    drive = (step_size * conv_float)[:, None, :] * in_map[:, :, None]
    out_wide = out_map[:, :, None]
    s_blk, a_blk = block_summary(decay, drive)
    state_in = entering_state(a_blk, s_blk, "seq")
    end_flag = ends_here.astype(jnp.int32)
    slot_of = jnp.minimum(prompt_of, prompts - 1).astype(jnp.int32)
    mixer_y, final_part = block_output(decay, drive, out_wide, state_in, end_flag, slot_of, prompts)
    mixer_y = mixer_y + d_skip[None, :] * conv_float
    gated = (mixer_y * jax.nn.silu(z_branch.astype(jnp.float32))).astype(jnp.bfloat16)
    ends_local = (prompt_end - 1 >= first_row) & (prompt_end - 1 < first_row + block_len)
    lag_ids = jnp.arange(edge_len, dtype=jnp.int32)
    ext_rows = jnp.arange(block_len + edge_len, dtype=jnp.int32)
    target_row = prompt_end[:, None] + lag_ids[None, :] - first_row
    inside = (
        prompt_end[:, None] - edge_len + lag_ids[None, :] >= prompt_start[:, None]
    ) & ends_local[:, None]
    edge_pick = ((ext_rows[None, None, :] == target_row[:, :, None]) & inside[:, :, None]).astype(
        jnp.bfloat16
    )
    edge_part = jnp.einsum("pji,ie->pje", edge_pick, extended, preferred_element_type=jnp.float32)
    handed = jnp.concatenate(
        [final_part.astype(jnp.bfloat16), edge_part.astype(jnp.bfloat16)], axis=1
    )
    handed = butterfly_sum(handed, "seq", jnp.bfloat16).astype(jnp.float32)
    final_all = handed[:, :state_dim]
    edge_all = handed[:, state_dim:]
    chooser = (request_prompt[:, None] == prompt_ids[None, :]).astype(jnp.float32)
    req_states = jnp.einsum("rp,pne->rne", chooser, final_all, precision=lax.Precision.HIGHEST)
    req_edges = jnp.einsum(
        "rp,pje->rje", chooser, edge_all, precision=lax.Precision.HIGHEST
    ).astype(jnp.bfloat16)
    mixed_rows = scatter_rows(
        jnp.dot(gated, w_out, preferred_element_type=jnp.float32).astype(jnp.bfloat16),
        "tp",
        jnp.bfloat16,
    )
    token_rows = lax.dynamic_slice_in_dim(tokens, tp_pos * row_count, row_count, 0)
    residual_rows = token_rows.astype(jnp.float32) + mixed_rows
    normed_rows = rms_norm(residual_rows, mlp_gain).astype(jnp.bfloat16)
    normed_two = gather_rows(normed_rows, "tp")
    gate_val = jnp.dot(normed_two, w_gate, preferred_element_type=jnp.float32)
    up_val = jnp.dot(normed_two, w_up, preferred_element_type=jnp.float32)
    hidden = (jax.nn.silu(gate_val) * up_val).astype(jnp.bfloat16)
    mlp_share = scatter_rows(
        jnp.dot(hidden, w_down, preferred_element_type=jnp.float32).astype(jnp.bfloat16),
        "tp",
        jnp.bfloat16,
    )
    live_rows = lax.dynamic_slice_in_dim(is_live, tp_pos * row_count, row_count, 0).astype(
        jnp.float32
    )
    mixed_out = ((residual_rows + mlp_share) * live_rows[:, None]).astype(jnp.bfloat16)
    return (mixed_out, req_states, req_edges)


def solution(mesh):
    placed = (
        P("seq", None),
        P(),
        P(None, "tp"),
        P(None, "tp"),
        P(None, "tp"),
        P("tp"),
        P("tp", None),
        P(None, "tp"),
        P("tp"),
        P(None, "tp"),
        P("tp"),
        P("tp", None),
        P(),
        P(None, "tp"),
        P(None, "tp"),
        P("tp", None),
        P(),
        P("seq"),
    )
    return jax.shard_map(
        local,
        mesh=mesh,
        in_specs=placed,
        out_specs=(P(("seq", "tp"), None), P("seq", None, "tp"), P("seq", None, "tp")),
        check_vma=False,
    )
```

```python
import functools

import jax
import jax.numpy as jnp
from jax import lax
from jax.experimental import pallas as pl
from jax.experimental.pallas import tpu as pltpu
from jax.sharding import PartitionSpec as P

EPSILON = 1e-05
INTERPRET = False


def from_behind(x, axis, by):
    devices = lax.axis_size(axis)
    pairs = [(i, i + by) for i in range(devices) if 0 <= i + by < devices]
    return lax.ppermute(x, axis, pairs)


def swap(x, axis, bit):
    devices = lax.axis_size(axis)
    return lax.ppermute(x, axis, [(i, i ^ bit) for i in range(devices)])


RINGS = {"seq": (8, 4), "tp": (4, 2)}


def ring_vectors(size):
    return {1: [], 2: [1], 4: [1, 3], 8: [1, 2, 6]}[size]


def basis_of(axis):
    devices = lax.axis_size(axis)
    rings = RINGS.get(axis, ())
    prod = 1
    for r in rings:
        prod *= r
    if prod != devices or any(r not in (1, 2, 4, 8) for r in rings):
        rings = (devices,)
    out = []
    shift = 0
    for r in reversed(rings):
        if r > 8:
            vecs = [1 << i for i in range(r.bit_length() - 1)]
            assert 1 << len(vecs) == r
        else:
            vecs = ring_vectors(r)
        for v in vecs:
            out.append((v << shift, (v << shift).bit_length() - 1))
        shift += len(vecs)
    assert 1 << shift == devices
    return out


def butterfly_sum(x, axis, send_dtype):
    for mask, _ in basis_of(axis):
        x = x + swap(x.astype(send_dtype), axis, mask).astype(x.dtype)
    return x


def scatter_order(axis):
    order = sorted(basis_of(axis), key=lambda vh: -vh[1])
    if order[-1] == (1, 0) and all(mask % 2 == 0 for mask, _ in order[:-1]):
        order = order[-1:] + order[:-1]
    return order


def scatter_rows(x, axis, first_dtype):
    devices = lax.axis_size(axis)
    me = lax.axis_index(axis)
    depth = devices.bit_length() - 1
    rows = x.shape[0] // devices
    buf = x.reshape((2,) * depth + (rows, x.shape[1]))
    left = list(range(depth - 1, -1, -1))
    send_dtype = first_dtype
    for mask, top in scatter_order(axis):
        at = left.index(top)
        mine = ((me // (1 << top)) % 2).astype(jnp.int32)
        keep = lax.dynamic_index_in_dim(buf, mine, at, False)
        give = lax.dynamic_index_in_dim(buf, 1 - mine, at, False)
        got = swap(give.astype(send_dtype), axis, mask)
        buf = keep.astype(jnp.float32) + got.astype(jnp.float32)
        left.remove(top)
    return buf


def gather_rows(x, axis):
    devices = lax.axis_size(axis)
    me = lax.axis_index(axis)
    buf = x
    held = []
    for mask, top in reversed(scatter_order(axis)):
        got = swap(buf, axis, mask)
        upper = ((me // (1 << top)) % 2) == 1
        low = jnp.where(upper, got, buf)
        high = jnp.where(upper, buf, got)
        at = sum(1 for b in held if b > top)
        buf = jnp.stack([low, high], axis=at)
        held.insert(at, top)
    return buf.reshape((devices * x.shape[0], x.shape[1]))


def rms_norm(values, gain):
    scale = lax.rsqrt(jnp.mean(values * values, axis=-1, keepdims=True) + EPSILON)
    return values * scale * gain


def block_summary_kernel(da_ref, dr_ref, send_ref, atot_ref):
    steps = da_ref.shape[0]

    def chunk(c, carry):
        state, acum = carry
        base = c * 8
        for i in range(8):
            da = da_ref[base + i]
            state = da * state + dr_ref[base + i]
            acum = da * acum
        return state, acum

    zero = jnp.zeros(send_ref.shape, jnp.float32)
    one = jnp.ones(atot_ref.shape, jnp.float32)
    state, acum = lax.fori_loop(0, steps // 8, chunk, (zero, one))
    send_ref[...] = state
    atot_ref[...] = acum


def block_output_kernel(da_ref, dr_ref, om_ref, sin_ref, endf_ref, pid_ref, y_ref, fin_ref):
    steps = da_ref.shape[0]
    width = y_ref.shape[1]
    fin_ref[...] = jnp.zeros(fin_ref.shape, jnp.float32)
    row_ids = lax.broadcasted_iota(jnp.int32, (8, width), 0)

    def chunk(c, state):
        base = pl.multiple_of(c * 8, 8)
        rows = jnp.zeros((8, width), jnp.float32)
        for i in range(8):
            t = base + i
            state = da_ref[t] * state + dr_ref[t]
            here = jnp.sum(om_ref[t] * state, axis=0, keepdims=True)
            rows = jnp.where(row_ids == i, here, rows)

            @pl.when(endf_ref[t] != 0)
            def _():
                fin_ref[pid_ref[t]] = state

        y_ref[pl.ds(base, 8), :] = rows
        return state

    lax.fori_loop(0, steps // 8, chunk, sin_ref[...])


def block_summary(da, dr):
    _, n, e = da.shape
    vmem = pl.BlockSpec(memory_space=pltpu.VMEM)
    return pl.pallas_call(
        block_summary_kernel,
        out_shape=(
            jax.ShapeDtypeStruct((n, e), jnp.float32),
            jax.ShapeDtypeStruct((n, e), jnp.float32),
        ),
        in_specs=[vmem, vmem],
        out_specs=(vmem, vmem),
        interpret=INTERPRET,
    )(da, dr)


def block_output(da, dr, om, sin, endf, pid, prompts):
    t, n, e = da.shape
    vmem = pl.BlockSpec(memory_space=pltpu.VMEM)
    smem = pl.BlockSpec(memory_space=pltpu.SMEM)
    return pl.pallas_call(
        block_output_kernel,
        out_shape=(
            jax.ShapeDtypeStruct((t, e), jnp.float32),
            jax.ShapeDtypeStruct((prompts, n, e), jnp.float32),
        ),
        in_specs=[vmem, vmem, vmem, vmem, smem, smem],
        out_specs=(vmem, vmem),
        interpret=INTERPRET,
    )(da, dr, om, sin, endf, pid)


def entering_state(a_blk, s_blk, axis, rider):
    me = lax.axis_index(axis)
    tot_a, tot_s = a_blk, s_blk
    exc_a, exc_s = jnp.ones_like(a_blk), jnp.zeros_like(s_blk)
    for mask, top in basis_of(axis):
        got = swap(jnp.stack([tot_a, tot_s]), axis, mask)
        if rider is not None:
            got, rider = lax.optimization_barrier((got, rider))
            rider_out, rider = rider, None
        got_a, got_s = got[0], got[1]
        upper = ((me // (1 << top)) % 2) == 1
        low_a = jnp.where(upper, got_a, tot_a)
        low_s = jnp.where(upper, got_s, tot_s)
        high_a = jnp.where(upper, tot_a, got_a)
        high_s = jnp.where(upper, tot_s, got_s)
        exc_a, exc_s = (
            jnp.where(upper, got_a * exc_a, exc_a),
            jnp.where(upper, exc_a * got_s + exc_s, exc_s),
        )
        tot_a, tot_s = low_a * high_a, high_a * low_s + high_s
    return exc_s, rider_out


def local(
    tokens,
    norm_gain,
    w_x,
    w_z,
    conv_w,
    conv_b,
    w_xproj,
    w_dt,
    dt_bias,
    a_log,
    d_skip,
    w_out,
    mlp_gain,
    w_gate,
    w_up,
    w_down,
    prompt_lengths,
    request_prompt,
):
    block_len = tokens.shape[0]
    tp_count = lax.axis_size("tp")
    row_count = block_len // tp_count
    seq_pos = lax.axis_index("seq")
    tp_pos = lax.axis_index("tp")
    first_row = seq_pos * block_len
    prompts = prompt_lengths.shape[0]
    kernel_len = conv_w.shape[0]
    edge_len = kernel_len - 1
    low_dim = w_dt.shape[0]
    state_dim = a_log.shape[0]
    chans = w_x.shape[1]
    places = first_row + jnp.arange(block_len, dtype=jnp.int32)
    prompt_end = jnp.cumsum(prompt_lengths)
    prompt_start = prompt_end - prompt_lengths
    prompt_ids = jnp.arange(prompts, dtype=jnp.int32)
    prompt_of = jnp.sum((places[:, None] >= prompt_end[None, :]).astype(jnp.int32), axis=1)
    start_of = jnp.sum(
        jnp.where(prompt_of[:, None] == prompt_ids[None, :], prompt_start[None, :], 0), axis=1
    )
    offset = places - start_of
    starts_here = jnp.any(places[:, None] == prompt_start[None, :], axis=1)
    ends_here = jnp.any(places[:, None] == prompt_end[None, :] - 1, axis=1)
    is_live = prompt_of < prompts
    seq_count = lax.axis_size("seq")
    behind = lax.ppermute(
        tokens[block_len - edge_len :],
        "seq",
        [(i, (i + 1) % seq_count) for i in range(seq_count)],
    )
    normed = rms_norm(tokens.astype(jnp.float32), norm_gain).astype(jnp.bfloat16)
    normed_behind = rms_norm(behind.astype(jnp.float32), norm_gain).astype(jnp.bfloat16)
    x_branch = jnp.dot(normed, w_x, preferred_element_type=jnp.float32).astype(jnp.bfloat16)
    z_branch = jnp.dot(normed, w_z, preferred_element_type=jnp.float32).astype(jnp.bfloat16)
    x_behind = jnp.dot(normed_behind, w_x, preferred_element_type=jnp.float32).astype(jnp.bfloat16)
    extended = jnp.concatenate([x_behind, x_branch], axis=0)
    conv_sum = jnp.zeros((block_len, chans), jnp.float32) + conv_b[None, :]
    for lag_steps in range(kernel_len):
        window = extended[edge_len - lag_steps : edge_len - lag_steps + block_len].astype(
            jnp.float32
        )
        reach_mask = (offset >= lag_steps).astype(jnp.float32)[:, None]
        conv_sum = conv_sum + conv_w[edge_len - lag_steps][None, :] * window * reach_mask
    conv_out = jax.nn.silu(conv_sum).astype(jnp.bfloat16)
    conv_float = conv_out.astype(jnp.float32)
    projected = butterfly_sum(
        jnp.dot(conv_out, w_xproj, preferred_element_type=jnp.float32), "tp", jnp.bfloat16
    )
    low_rank = projected[:, :low_dim].astype(jnp.bfloat16)
    in_map = projected[:, low_dim : low_dim + state_dim]
    out_map = projected[:, low_dim + state_dim :]
    step_size = jax.nn.softplus(
        jnp.dot(low_rank, w_dt, preferred_element_type=jnp.float32) + dt_bias[None, :]
    )
    decay_rates = -jnp.exp(a_log)
    carry_on = 1.0 - starts_here.astype(jnp.float32)
    decay = jnp.exp(step_size[:, None, :] * decay_rates[None, :, :]) * carry_on[:, None, None]
    drive = (step_size * conv_float)[:, None, :] * in_map[:, :, None]
    out_wide = jnp.broadcast_to(out_map[:, :, None], decay.shape)
    s_blk, a_blk = block_summary(decay, drive)
    state_in, out_wide = entering_state(a_blk, s_blk, "seq", out_wide)
    end_flag = ends_here.astype(jnp.int32)
    slot_of = jnp.minimum(prompt_of, prompts - 1).astype(jnp.int32)
    mixer_y, final_part = block_output(decay, drive, out_wide, state_in, end_flag, slot_of, prompts)
    mixer_y = mixer_y + d_skip[None, :] * conv_float
    gated = (mixer_y * jax.nn.silu(z_branch.astype(jnp.float32))).astype(jnp.bfloat16)
    ends_local = (prompt_end - 1 >= first_row) & (prompt_end - 1 < first_row + block_len)
    lag_ids = jnp.arange(edge_len, dtype=jnp.int32)
    ext_rows = jnp.arange(block_len + edge_len, dtype=jnp.int32)
    target_row = prompt_end[:, None] + lag_ids[None, :] - first_row
    inside = (
        prompt_end[:, None] - edge_len + lag_ids[None, :] >= prompt_start[:, None]
    ) & ends_local[:, None]
    edge_pick = ((ext_rows[None, None, :] == target_row[:, :, None]) & inside[:, :, None]).astype(
        jnp.bfloat16
    )
    edge_part = jnp.einsum("pji,ie->pje", edge_pick, extended, preferred_element_type=jnp.float32)
    handed = jnp.concatenate(
        [final_part.astype(jnp.bfloat16), edge_part.astype(jnp.bfloat16)], axis=1
    )
    handed = butterfly_sum(handed, "seq", jnp.bfloat16).astype(jnp.float32)
    final_all = handed[:, :state_dim]
    edge_all = handed[:, state_dim:]
    chooser = (request_prompt[:, None] == prompt_ids[None, :]).astype(jnp.float32)
    req_states = jnp.einsum("rp,pne->rne", chooser, final_all, precision=lax.Precision.HIGHEST)
    req_edges = jnp.einsum(
        "rp,pje->rje", chooser, edge_all, precision=lax.Precision.HIGHEST
    ).astype(jnp.bfloat16)
    mixed_rows = scatter_rows(
        jnp.dot(gated, w_out, preferred_element_type=jnp.float32).astype(jnp.bfloat16),
        "tp",
        jnp.bfloat16,
    )
    token_rows = lax.dynamic_slice_in_dim(tokens, tp_pos * row_count, row_count, 0)
    residual_rows = token_rows.astype(jnp.float32) + mixed_rows
    normed_rows = rms_norm(residual_rows, mlp_gain).astype(jnp.bfloat16)
    normed_two = gather_rows(normed_rows, "tp")
    gate_val = jnp.dot(normed_two, w_gate, preferred_element_type=jnp.float32)
    up_val = jnp.dot(normed_two, w_up, preferred_element_type=jnp.float32)
    hidden = (jax.nn.silu(gate_val) * up_val).astype(jnp.bfloat16)
    mlp_share = scatter_rows(
        jnp.dot(hidden, w_down, preferred_element_type=jnp.float32).astype(jnp.bfloat16),
        "tp",
        jnp.bfloat16,
    )
    live_rows = lax.dynamic_slice_in_dim(is_live, tp_pos * row_count, row_count, 0).astype(
        jnp.float32
    )
    mixed_out = ((residual_rows + mlp_share) * live_rows[:, None]).astype(jnp.bfloat16)
    return (mixed_out, req_states, req_edges)


def solution(mesh):
    placed = (
        P("seq", None),
        P(),
        P(None, "tp"),
        P(None, "tp"),
        P(None, "tp"),
        P("tp"),
        P("tp", None),
        P(None, "tp"),
        P("tp"),
        P(None, "tp"),
        P("tp"),
        P("tp", None),
        P(),
        P(None, "tp"),
        P(None, "tp"),
        P("tp", None),
        P(),
        P("seq"),
    )
    return jax.shard_map(
        local,
        mesh=mesh,
        in_specs=placed,
        out_specs=(P(("seq", "tp"), None), P("seq", None, "tp"), P("seq", None, "tp")),
        check_vma=False,
    )
```

```python
import functools

import jax
import jax.numpy as jnp
from jax import lax
from jax.experimental import pallas as pl
from jax.experimental.pallas import tpu as pltpu
from jax.sharding import PartitionSpec as P

EPSILON = 1e-05
INTERPRET = False


def from_behind(x, axis, by):
    devices = lax.axis_size(axis)
    pairs = [(i, i + by) for i in range(devices) if 0 <= i + by < devices]
    return lax.ppermute(x, axis, pairs)


def swap(x, axis, bit):
    devices = lax.axis_size(axis)
    return lax.ppermute(x, axis, [(i, i ^ bit) for i in range(devices)])


RINGS = {"seq": (8, 4), "tp": (4, 2)}


def ring_vectors(size):
    return {1: [], 2: [1], 4: [1, 3], 8: [1, 2, 6]}[size]


def basis_of(axis):
    devices = lax.axis_size(axis)
    rings = RINGS.get(axis, ())
    prod = 1
    for r in rings:
        prod *= r
    if prod != devices or any(r not in (1, 2, 4, 8) for r in rings):
        rings = (devices,)
    out = []
    shift = 0
    for r in reversed(rings):
        if r > 8:
            vecs = [1 << i for i in range(r.bit_length() - 1)]
            assert 1 << len(vecs) == r
        else:
            vecs = ring_vectors(r)
        for v in vecs:
            out.append((v << shift, (v << shift).bit_length() - 1))
        shift += len(vecs)
    assert 1 << shift == devices
    return out


def butterfly_sum(x, axis, send_dtype):
    for mask, _ in basis_of(axis):
        x = x + swap(x.astype(send_dtype), axis, mask).astype(x.dtype)
    return x


def scatter_order(axis):
    order = sorted(basis_of(axis), key=lambda vh: -vh[1])
    if order[-1] == (1, 0) and all(mask % 2 == 0 for mask, _ in order[:-1]):
        order = order[-1:] + order[:-1]
    return order


def scatter_rows(x, axis, first_dtype):
    devices = lax.axis_size(axis)
    me = lax.axis_index(axis)
    depth = devices.bit_length() - 1
    rows = x.shape[0] // devices
    buf = x.reshape((2,) * depth + (rows, x.shape[1]))
    left = list(range(depth - 1, -1, -1))
    send_dtype = first_dtype
    for mask, top in scatter_order(axis):
        at = left.index(top)
        mine = ((me // (1 << top)) % 2).astype(jnp.int32)
        keep = lax.dynamic_index_in_dim(buf, mine, at, False)
        give = lax.dynamic_index_in_dim(buf, 1 - mine, at, False)
        got = swap(give.astype(send_dtype), axis, mask)
        buf = keep.astype(jnp.float32) + got.astype(jnp.float32)
        left.remove(top)
    return buf


def gather_rows(x, axis):
    devices = lax.axis_size(axis)
    me = lax.axis_index(axis)
    buf = x
    held = []
    for mask, top in reversed(scatter_order(axis)):
        got = swap(buf, axis, mask)
        upper = ((me // (1 << top)) % 2) == 1
        low = jnp.where(upper, got, buf)
        high = jnp.where(upper, buf, got)
        at = sum(1 for b in held if b > top)
        buf = jnp.stack([low, high], axis=at)
        held.insert(at, top)
    return buf.reshape((devices * x.shape[0], x.shape[1]))


def rms_norm(values, gain):
    scale = lax.rsqrt(jnp.mean(values * values, axis=-1, keepdims=True) + EPSILON)
    return values * scale * gain


def block_summary_kernel(da_ref, dr_ref, send_ref, atot_ref):
    steps = da_ref.shape[0]

    def chunk(c, carry):
        state, acum = carry
        base = c * 8
        for i in range(8):
            da = da_ref[base + i]
            state = da * state + dr_ref[base + i]
            acum = da * acum
        return state, acum

    zero = jnp.zeros(send_ref.shape, jnp.float32)
    one = jnp.ones(atot_ref.shape, jnp.float32)
    state, acum = lax.fori_loop(0, steps // 8, chunk, (zero, one))
    send_ref[...] = state
    atot_ref[...] = acum


def block_output_kernel(da_ref, dr_ref, sin_ref, endf_ref, pid_ref, st_ref, fin_ref):
    steps = da_ref.shape[0]
    fin_ref[...] = jnp.zeros(fin_ref.shape, jnp.float32)

    def chunk(c, state):
        base = c * 8
        for i in range(8):
            t = base + i
            state = da_ref[t] * state + dr_ref[t]
            st_ref[t] = state

            @pl.when(endf_ref[t] != 0)
            def _():
                fin_ref[pid_ref[t]] = state

        return state

    lax.fori_loop(0, steps // 8, chunk, sin_ref[...])


def block_summary(da, dr):
    _, n, e = da.shape
    vmem = pl.BlockSpec(memory_space=pltpu.VMEM)
    return pl.pallas_call(
        block_summary_kernel,
        out_shape=(
            jax.ShapeDtypeStruct((n, e), jnp.float32),
            jax.ShapeDtypeStruct((n, e), jnp.float32),
        ),
        in_specs=[vmem, vmem],
        out_specs=(vmem, vmem),
        interpret=INTERPRET,
    )(da, dr)


def block_output(da, dr, sin, endf, pid, prompts):
    t, n, e = da.shape
    vmem = pl.BlockSpec(memory_space=pltpu.VMEM)
    smem = pl.BlockSpec(memory_space=pltpu.SMEM)
    return pl.pallas_call(
        block_output_kernel,
        out_shape=(
            jax.ShapeDtypeStruct((t, n, e), jnp.float32),
            jax.ShapeDtypeStruct((prompts, n, e), jnp.float32),
        ),
        in_specs=[vmem, vmem, vmem, smem, smem],
        out_specs=(vmem, vmem),
        interpret=INTERPRET,
    )(da, dr, sin, endf, pid)


def entering_state(a_blk, s_blk, axis, rider):
    me = lax.axis_index(axis)
    tot_a, tot_s = a_blk, s_blk
    exc_a, exc_s = jnp.ones_like(a_blk), jnp.zeros_like(s_blk)
    rider_out = None
    for mask, top in basis_of(axis):
        got = swap(jnp.stack([tot_a, tot_s]), axis, mask)
        if rider is not None:
            got, rider = lax.optimization_barrier((got, rider))
            rider_out, rider = rider, None
        got_a, got_s = got[0], got[1]
        upper = ((me // (1 << top)) % 2) == 1
        low_a = jnp.where(upper, got_a, tot_a)
        low_s = jnp.where(upper, got_s, tot_s)
        high_a = jnp.where(upper, tot_a, got_a)
        high_s = jnp.where(upper, tot_s, got_s)
        exc_a, exc_s = (
            jnp.where(upper, got_a * exc_a, exc_a),
            jnp.where(upper, exc_a * got_s + exc_s, exc_s),
        )
        tot_a, tot_s = low_a * high_a, high_a * low_s + high_s
    return exc_s, rider_out


def local(
    tokens,
    norm_gain,
    w_x,
    w_z,
    conv_w,
    conv_b,
    w_xproj,
    w_dt,
    dt_bias,
    a_log,
    d_skip,
    w_out,
    mlp_gain,
    w_gate,
    w_up,
    w_down,
    prompt_lengths,
    request_prompt,
):
    block_len = tokens.shape[0]
    tp_count = lax.axis_size("tp")
    row_count = block_len // tp_count
    seq_pos = lax.axis_index("seq")
    tp_pos = lax.axis_index("tp")
    first_row = seq_pos * block_len
    prompts = prompt_lengths.shape[0]
    kernel_len = conv_w.shape[0]
    edge_len = kernel_len - 1
    low_dim = w_dt.shape[0]
    state_dim = a_log.shape[0]
    chans = w_x.shape[1]
    places = first_row + jnp.arange(block_len, dtype=jnp.int32)
    prompt_end = jnp.cumsum(prompt_lengths)
    prompt_start = prompt_end - prompt_lengths
    prompt_ids = jnp.arange(prompts, dtype=jnp.int32)
    prompt_of = jnp.sum((places[:, None] >= prompt_end[None, :]).astype(jnp.int32), axis=1)
    start_of = jnp.sum(
        jnp.where(prompt_of[:, None] == prompt_ids[None, :], prompt_start[None, :], 0), axis=1
    )
    offset = places - start_of
    starts_here = jnp.any(places[:, None] == prompt_start[None, :], axis=1)
    ends_here = jnp.any(places[:, None] == prompt_end[None, :] - 1, axis=1)
    is_live = prompt_of < prompts
    seq_count = lax.axis_size("seq")
    behind = lax.ppermute(
        tokens[block_len - edge_len :],
        "seq",
        [(i, (i + 1) % seq_count) for i in range(seq_count)],
    )
    normed = rms_norm(tokens.astype(jnp.float32), norm_gain).astype(jnp.bfloat16)
    normed_behind = rms_norm(behind.astype(jnp.float32), norm_gain).astype(jnp.bfloat16)
    x_branch = jnp.dot(normed, w_x, preferred_element_type=jnp.float32).astype(jnp.bfloat16)
    z_branch = jnp.dot(normed, w_z, preferred_element_type=jnp.float32).astype(jnp.bfloat16)
    x_behind = jnp.dot(normed_behind, w_x, preferred_element_type=jnp.float32).astype(jnp.bfloat16)
    extended = jnp.concatenate([x_behind, x_branch], axis=0)
    conv_sum = jnp.zeros((block_len, chans), jnp.float32) + conv_b[None, :]
    for lag_steps in range(kernel_len):
        window = extended[edge_len - lag_steps : edge_len - lag_steps + block_len].astype(
            jnp.float32
        )
        reach_mask = (offset >= lag_steps).astype(jnp.float32)[:, None]
        conv_sum = conv_sum + conv_w[edge_len - lag_steps][None, :] * window * reach_mask
    conv_out = jax.nn.silu(conv_sum).astype(jnp.bfloat16)
    conv_float = conv_out.astype(jnp.float32)
    projected = butterfly_sum(
        jnp.dot(conv_out, w_xproj, preferred_element_type=jnp.float32), "tp", jnp.bfloat16
    )
    low_rank = projected[:, :low_dim].astype(jnp.bfloat16)
    in_map = projected[:, low_dim : low_dim + state_dim]
    out_map = projected[:, low_dim + state_dim :]
    step_size = jax.nn.softplus(
        jnp.dot(low_rank, w_dt, preferred_element_type=jnp.float32) + dt_bias[None, :]
    )
    decay_rates = -jnp.exp(a_log)
    carry_on = 1.0 - starts_here.astype(jnp.float32)
    decay = jnp.exp(step_size[:, None, :] * decay_rates[None, :, :]) * carry_on[:, None, None]
    drive = (step_size * conv_float)[:, None, :] * in_map[:, :, None]
    s_blk, a_blk = block_summary(decay, drive)
    state_in, _ = entering_state(a_blk, s_blk, "seq", None)
    end_flag = ends_here.astype(jnp.int32)
    slot_of = jnp.minimum(prompt_of, prompts - 1).astype(jnp.int32)
    states, final_part = block_output(decay, drive, state_in, end_flag, slot_of, prompts)
    mixer_y = jnp.sum(out_map[:, :, None] * states, axis=1)
    mixer_y = mixer_y + d_skip[None, :] * conv_float
    gated = (mixer_y * jax.nn.silu(z_branch.astype(jnp.float32))).astype(jnp.bfloat16)
    ends_local = (prompt_end - 1 >= first_row) & (prompt_end - 1 < first_row + block_len)
    lag_ids = jnp.arange(edge_len, dtype=jnp.int32)
    ext_rows = jnp.arange(block_len + edge_len, dtype=jnp.int32)
    target_row = prompt_end[:, None] + lag_ids[None, :] - first_row
    inside = (
        prompt_end[:, None] - edge_len + lag_ids[None, :] >= prompt_start[:, None]
    ) & ends_local[:, None]
    edge_pick = ((ext_rows[None, None, :] == target_row[:, :, None]) & inside[:, :, None]).astype(
        jnp.bfloat16
    )
    edge_part = jnp.einsum("pji,ie->pje", edge_pick, extended, preferred_element_type=jnp.float32)
    handed = jnp.concatenate(
        [final_part.astype(jnp.bfloat16), edge_part.astype(jnp.bfloat16)], axis=1
    )
    handed = butterfly_sum(handed, "seq", jnp.bfloat16).astype(jnp.float32)
    final_all = handed[:, :state_dim]
    edge_all = handed[:, state_dim:]
    chooser = (request_prompt[:, None] == prompt_ids[None, :]).astype(jnp.float32)
    req_states = jnp.einsum("rp,pne->rne", chooser, final_all, precision=lax.Precision.HIGHEST)
    req_edges = jnp.einsum(
        "rp,pje->rje", chooser, edge_all, precision=lax.Precision.HIGHEST
    ).astype(jnp.bfloat16)
    mixed_rows = scatter_rows(
        jnp.dot(gated, w_out, preferred_element_type=jnp.float32).astype(jnp.bfloat16),
        "tp",
        jnp.bfloat16,
    )
    token_rows = lax.dynamic_slice_in_dim(tokens, tp_pos * row_count, row_count, 0)
    residual_rows = token_rows.astype(jnp.float32) + mixed_rows
    normed_rows = rms_norm(residual_rows, mlp_gain).astype(jnp.bfloat16)
    normed_two = gather_rows(normed_rows, "tp")
    gate_val = jnp.dot(normed_two, w_gate, preferred_element_type=jnp.float32)
    up_val = jnp.dot(normed_two, w_up, preferred_element_type=jnp.float32)
    hidden = (jax.nn.silu(gate_val) * up_val).astype(jnp.bfloat16)
    mlp_share = scatter_rows(
        jnp.dot(hidden, w_down, preferred_element_type=jnp.float32).astype(jnp.bfloat16),
        "tp",
        jnp.bfloat16,
    )
    live_rows = lax.dynamic_slice_in_dim(is_live, tp_pos * row_count, row_count, 0).astype(
        jnp.float32
    )
    mixed_out = ((residual_rows + mlp_share) * live_rows[:, None]).astype(jnp.bfloat16)
    return (mixed_out, req_states, req_edges)


def solution(mesh):
    placed = (
        P("seq", None),
        P(),
        P(None, "tp"),
        P(None, "tp"),
        P(None, "tp"),
        P("tp"),
        P("tp", None),
        P(None, "tp"),
        P("tp"),
        P(None, "tp"),
        P("tp"),
        P("tp", None),
        P(),
        P(None, "tp"),
        P(None, "tp"),
        P("tp", None),
        P(),
        P("seq"),
    )
    return jax.shard_map(
        local,
        mesh=mesh,
        in_specs=placed,
        out_specs=(P(("seq", "tp"), None), P("seq", None, "tp"), P("seq", None, "tp")),
        check_vma=False,
    )
```

```python
import functools

import jax
import jax.numpy as jnp
from jax import lax
from jax.experimental import pallas as pl
from jax.experimental.pallas import tpu as pltpu
from jax.sharding import PartitionSpec as P

EPSILON = 1e-05
INTERPRET = False


def from_behind(x, axis, by):
    devices = lax.axis_size(axis)
    pairs = [(i, i + by) for i in range(devices) if 0 <= i + by < devices]
    return lax.ppermute(x, axis, pairs)


def swap(x, axis, bit):
    devices = lax.axis_size(axis)
    return lax.ppermute(x, axis, [(i, i ^ bit) for i in range(devices)])


RINGS = {"seq": (8, 4), "tp": (4, 2)}


def ring_vectors(size):
    return {1: [], 2: [1], 4: [1, 3], 8: [1, 2, 6]}[size]


def basis_of(axis):
    devices = lax.axis_size(axis)
    rings = RINGS.get(axis, ())
    prod = 1
    for r in rings:
        prod *= r
    if prod != devices or any(r not in (1, 2, 4, 8) for r in rings):
        rings = (devices,)
    out = []
    shift = 0
    for r in reversed(rings):
        if r > 8:
            vecs = [1 << i for i in range(r.bit_length() - 1)]
            assert 1 << len(vecs) == r
        else:
            vecs = ring_vectors(r)
        for v in vecs:
            out.append((v << shift, (v << shift).bit_length() - 1))
        shift += len(vecs)
    assert 1 << shift == devices
    return out


def butterfly_sum(x, axis, send_dtype):
    for mask, _ in basis_of(axis):
        x = x + swap(x.astype(send_dtype), axis, mask).astype(x.dtype)
    return x


def scatter_order(axis):
    order = sorted(basis_of(axis), key=lambda vh: -vh[1])
    if order[-1] == (1, 0) and all(mask % 2 == 0 for mask, _ in order[:-1]):
        order = order[-1:] + order[:-1]
    return order


def scatter_rows(x, axis, first_dtype):
    devices = lax.axis_size(axis)
    me = lax.axis_index(axis)
    depth = devices.bit_length() - 1
    rows = x.shape[0] // devices
    buf = x.reshape((2,) * depth + (rows, x.shape[1]))
    left = list(range(depth - 1, -1, -1))
    send_dtype = first_dtype
    for mask, top in scatter_order(axis):
        at = left.index(top)
        mine = ((me // (1 << top)) % 2).astype(jnp.int32)
        keep = lax.dynamic_index_in_dim(buf, mine, at, False)
        give = lax.dynamic_index_in_dim(buf, 1 - mine, at, False)
        got = swap(give.astype(send_dtype), axis, mask)
        buf = keep.astype(jnp.float32) + got.astype(jnp.float32)
        left.remove(top)
    return buf


def gather_rows(x, axis):
    devices = lax.axis_size(axis)
    me = lax.axis_index(axis)
    buf = x
    held = []
    for mask, top in reversed(scatter_order(axis)):
        got = swap(buf, axis, mask)
        upper = ((me // (1 << top)) % 2) == 1
        low = jnp.where(upper, got, buf)
        high = jnp.where(upper, buf, got)
        at = sum(1 for b in held if b > top)
        buf = jnp.stack([low, high], axis=at)
        held.insert(at, top)
    return buf.reshape((devices * x.shape[0], x.shape[1]))


def rms_norm(values, gain):
    scale = lax.rsqrt(jnp.mean(values * values, axis=-1, keepdims=True) + EPSILON)
    return values * scale * gain


def block_summary_kernel(da_ref, dr_ref, send_ref, atot_ref):
    steps = da_ref.shape[0]

    def chunk(c, carry):
        state, acum = carry
        base = c * 8
        for i in range(8):
            da = da_ref[base + i]
            state = da * state + dr_ref[base + i]
            acum = da * acum
        return state, acum

    zero = jnp.zeros(send_ref.shape, jnp.float32)
    one = jnp.ones(atot_ref.shape, jnp.float32)
    state, acum = lax.fori_loop(0, steps // 8, chunk, (zero, one))
    send_ref[...] = state
    atot_ref[...] = acum


def block_output_kernel(da_ref, dr_ref, om_ref, sin_ref, endf_ref, pid_ref, y_ref, fin_ref):
    steps = da_ref.shape[0]
    width = y_ref.shape[1]
    fin_ref[...] = jnp.zeros(fin_ref.shape, jnp.float32)
    row_ids = lax.broadcasted_iota(jnp.int32, (8, width), 0)

    def chunk(c, state):
        base = pl.multiple_of(c * 8, 8)
        rows = jnp.zeros((8, width), jnp.float32)
        for i in range(8):
            t = base + i
            state = da_ref[t] * state + dr_ref[t]
            here = jnp.sum(om_ref[t] * state, axis=0, keepdims=True)
            rows = jnp.where(row_ids == i, here, rows)

            @pl.when(endf_ref[t] != 0)
            def _():
                fin_ref[pid_ref[t]] = state

        y_ref[pl.ds(base, 8), :] = rows
        return state

    lax.fori_loop(0, steps // 8, chunk, sin_ref[...])


def block_summary(da, dr):
    _, n, e = da.shape
    vmem = pl.BlockSpec(memory_space=pltpu.VMEM)
    return pl.pallas_call(
        block_summary_kernel,
        out_shape=(
            jax.ShapeDtypeStruct((n, e), jnp.float32),
            jax.ShapeDtypeStruct((n, e), jnp.float32),
        ),
        in_specs=[vmem, vmem],
        out_specs=(vmem, vmem),
        interpret=INTERPRET,
    )(da, dr)


def block_output(da, dr, om, sin, endf, pid, prompts):
    t, n, e = da.shape
    vmem = pl.BlockSpec(memory_space=pltpu.VMEM)
    smem = pl.BlockSpec(memory_space=pltpu.SMEM)
    return pl.pallas_call(
        block_output_kernel,
        out_shape=(
            jax.ShapeDtypeStruct((t, e), jnp.float32),
            jax.ShapeDtypeStruct((prompts, n, e), jnp.float32),
        ),
        in_specs=[vmem, vmem, vmem, vmem, smem, smem],
        out_specs=(vmem, vmem),
        interpret=INTERPRET,
    )(da, dr, om, sin, endf, pid)


def entering_state(a_blk, s_blk, axis, rider):
    me = lax.axis_index(axis)
    tot_a, tot_s = a_blk, s_blk
    exc_a, exc_s = jnp.ones_like(a_blk), jnp.zeros_like(s_blk)
    rider_out = None
    for mask, top in basis_of(axis):
        got = swap(jnp.stack([tot_a, tot_s]), axis, mask)
        if rider is not None:
            got, rider = lax.optimization_barrier((got, rider))
            rider_out, rider = rider, None
        got_a, got_s = got[0], got[1]
        upper = ((me // (1 << top)) % 2) == 1
        low_a = jnp.where(upper, got_a, tot_a)
        low_s = jnp.where(upper, got_s, tot_s)
        high_a = jnp.where(upper, tot_a, got_a)
        high_s = jnp.where(upper, tot_s, got_s)
        exc_a, exc_s = (
            jnp.where(upper, got_a * exc_a, exc_a),
            jnp.where(upper, exc_a * got_s + exc_s, exc_s),
        )
        tot_a, tot_s = low_a * high_a, high_a * low_s + high_s
    return exc_s, rider_out


def local(
    tokens,
    norm_gain,
    w_x,
    w_z,
    conv_w,
    conv_b,
    w_xproj,
    w_dt,
    dt_bias,
    a_log,
    d_skip,
    w_out,
    mlp_gain,
    w_gate,
    w_up,
    w_down,
    prompt_lengths,
    request_prompt,
):
    block_len = tokens.shape[0]
    tp_count = lax.axis_size("tp")
    row_count = block_len // tp_count
    seq_pos = lax.axis_index("seq")
    tp_pos = lax.axis_index("tp")
    first_row = seq_pos * block_len
    prompts = prompt_lengths.shape[0]
    kernel_len = conv_w.shape[0]
    edge_len = kernel_len - 1
    low_dim = w_dt.shape[0]
    state_dim = a_log.shape[0]
    chans = w_x.shape[1]
    places = first_row + jnp.arange(block_len, dtype=jnp.int32)
    prompt_end = jnp.cumsum(prompt_lengths)
    prompt_start = prompt_end - prompt_lengths
    prompt_ids = jnp.arange(prompts, dtype=jnp.int32)
    prompt_of = jnp.sum((places[:, None] >= prompt_end[None, :]).astype(jnp.int32), axis=1)
    start_of = jnp.sum(
        jnp.where(prompt_of[:, None] == prompt_ids[None, :], prompt_start[None, :], 0), axis=1
    )
    offset = places - start_of
    starts_here = jnp.any(places[:, None] == prompt_start[None, :], axis=1)
    ends_here = jnp.any(places[:, None] == prompt_end[None, :] - 1, axis=1)
    is_live = prompt_of < prompts
    seq_count = lax.axis_size("seq")
    behind = lax.ppermute(
        tokens[block_len - edge_len :],
        "seq",
        [(i, (i + 1) % seq_count) for i in range(seq_count)],
    )
    normed = rms_norm(tokens.astype(jnp.float32), norm_gain).astype(jnp.bfloat16)
    normed_behind = rms_norm(behind.astype(jnp.float32), norm_gain).astype(jnp.bfloat16)
    x_branch = jnp.dot(normed, w_x, preferred_element_type=jnp.float32).astype(jnp.bfloat16)
    z_branch = jnp.dot(normed, w_z, preferred_element_type=jnp.float32).astype(jnp.bfloat16)
    x_behind = jnp.dot(normed_behind, w_x, preferred_element_type=jnp.float32).astype(jnp.bfloat16)
    extended = jnp.concatenate([x_behind, x_branch], axis=0)
    conv_sum = jnp.zeros((block_len, chans), jnp.float32) + conv_b[None, :]
    for lag_steps in range(kernel_len):
        window = extended[edge_len - lag_steps : edge_len - lag_steps + block_len].astype(
            jnp.float32
        )
        reach_mask = (offset >= lag_steps).astype(jnp.float32)[:, None]
        conv_sum = conv_sum + conv_w[edge_len - lag_steps][None, :] * window * reach_mask
    conv_out = jax.nn.silu(conv_sum).astype(jnp.bfloat16)
    conv_float = conv_out.astype(jnp.float32)
    projected = butterfly_sum(
        jnp.dot(conv_out, w_xproj, preferred_element_type=jnp.float32), "tp", jnp.bfloat16
    )
    low_rank = projected[:, :low_dim].astype(jnp.bfloat16)
    in_map = projected[:, low_dim : low_dim + state_dim]
    out_map = projected[:, low_dim + state_dim :]
    step_size = jax.nn.softplus(
        jnp.dot(low_rank, w_dt, preferred_element_type=jnp.float32) + dt_bias[None, :]
    )
    decay_rates = -jnp.exp(a_log)
    carry_on = 1.0 - starts_here.astype(jnp.float32)
    decay = jnp.exp(step_size[:, None, :] * decay_rates[None, :, :]) * carry_on[:, None, None]
    drive = (step_size * conv_float)[:, None, :] * in_map[:, :, None]
    out_wide = out_map[:, :, None] + 0.0 * decay
    s_blk, a_blk = block_summary(decay, drive)
    state_in, _ = entering_state(a_blk, s_blk, "seq", None)
    end_flag = ends_here.astype(jnp.int32)
    slot_of = jnp.minimum(prompt_of, prompts - 1).astype(jnp.int32)
    mixer_y, final_part = block_output(decay, drive, out_wide, state_in, end_flag, slot_of, prompts)
    mixer_y = mixer_y + d_skip[None, :] * conv_float
    gated = (mixer_y * jax.nn.silu(z_branch.astype(jnp.float32))).astype(jnp.bfloat16)
    ends_local = (prompt_end - 1 >= first_row) & (prompt_end - 1 < first_row + block_len)
    lag_ids = jnp.arange(edge_len, dtype=jnp.int32)
    ext_rows = jnp.arange(block_len + edge_len, dtype=jnp.int32)
    target_row = prompt_end[:, None] + lag_ids[None, :] - first_row
    inside = (
        prompt_end[:, None] - edge_len + lag_ids[None, :] >= prompt_start[:, None]
    ) & ends_local[:, None]
    edge_pick = ((ext_rows[None, None, :] == target_row[:, :, None]) & inside[:, :, None]).astype(
        jnp.bfloat16
    )
    edge_part = jnp.einsum("pji,ie->pje", edge_pick, extended, preferred_element_type=jnp.float32)
    handed = jnp.concatenate(
        [final_part.astype(jnp.bfloat16), edge_part.astype(jnp.bfloat16)], axis=1
    )
    handed = butterfly_sum(handed, "seq", jnp.bfloat16).astype(jnp.float32)
    final_all = handed[:, :state_dim]
    edge_all = handed[:, state_dim:]
    chooser = (request_prompt[:, None] == prompt_ids[None, :]).astype(jnp.float32)
    req_states = jnp.einsum("rp,pne->rne", chooser, final_all, precision=lax.Precision.HIGHEST)
    req_edges = jnp.einsum(
        "rp,pje->rje", chooser, edge_all, precision=lax.Precision.HIGHEST
    ).astype(jnp.bfloat16)
    mixed_rows = scatter_rows(
        jnp.dot(gated, w_out, preferred_element_type=jnp.float32).astype(jnp.bfloat16),
        "tp",
        jnp.bfloat16,
    )
    token_rows = lax.dynamic_slice_in_dim(tokens, tp_pos * row_count, row_count, 0)
    residual_rows = token_rows.astype(jnp.float32) + mixed_rows
    normed_rows = rms_norm(residual_rows, mlp_gain).astype(jnp.bfloat16)
    normed_two = gather_rows(normed_rows, "tp")
    gate_val = jnp.dot(normed_two, w_gate, preferred_element_type=jnp.float32)
    up_val = jnp.dot(normed_two, w_up, preferred_element_type=jnp.float32)
    hidden = (jax.nn.silu(gate_val) * up_val).astype(jnp.bfloat16)
    mlp_share = scatter_rows(
        jnp.dot(hidden, w_down, preferred_element_type=jnp.float32).astype(jnp.bfloat16),
        "tp",
        jnp.bfloat16,
    )
    live_rows = lax.dynamic_slice_in_dim(is_live, tp_pos * row_count, row_count, 0).astype(
        jnp.float32
    )
    mixed_out = ((residual_rows + mlp_share) * live_rows[:, None]).astype(jnp.bfloat16)
    return (mixed_out, req_states, req_edges)


def solution(mesh):
    placed = (
        P("seq", None),
        P(),
        P(None, "tp"),
        P(None, "tp"),
        P(None, "tp"),
        P("tp"),
        P("tp", None),
        P(None, "tp"),
        P("tp"),
        P(None, "tp"),
        P("tp"),
        P("tp", None),
        P(),
        P(None, "tp"),
        P(None, "tp"),
        P("tp", None),
        P(),
        P("seq"),
    )
    return jax.shard_map(
        local,
        mesh=mesh,
        in_specs=placed,
        out_specs=(P(("seq", "tp"), None), P("seq", None, "tp"), P("seq", None, "tp")),
        check_vma=False,
    )
```
